512 devices in a mesh: clus: 256 (over z, y, x), samp: 2 (over core).
Axes of the slice: x: 4, y: 8, z: 8, core: 2. Of those that a mesh axis runs over, the one named last changes fastest.
Arguments:
- samples: float32 [262144, 256], P('clus', 'samp'), may hold values from -8 to 8
- sketch: float32 [256, 128], P('samp'), may hold values from -0.375 to 0.375
- leaf_slot: int32 [256, 4], P('clus'), may hold values from 0 to 3, each once within a row
Outputs:
- leaf_basis: float32 [262144, 128], P('clus')
- local_transfer: float32 [768, 256, 128], P('clus')
- top_transfer: float32 [256, 256, 128], P('clus')
- root_factor: float32 [128, 128], replicated
The draws below stay inside these ranges and needn't reach their ends.
Inputs may be any that keep to these rules, and one draw needn't show every extreme that they name: Each row of leaf_slot names every number from 0 to 3 once.
All inputs are finite; a program needn't handle non-finite values.
Results may differ from the reference program's by a relative error of at most 0.0003.
Values sent between devices are 32-bit elements; how exact they have to be, the bound alone decides.
No kernel may reach another device: no remote copies, remote signals or barrier semaphores. Data moves between devices by JAX's collectives and lax.ppermute only.
A program may use at most 64 MiB of HBM per device.

```python
import jax
import jax.numpy as jnp
from jax import lax

K = 128
S = 256
LEAF = 256
NS_STEPS = 5
LEAVES_DEV = 4
LEAVES = 1024
ROWS = 262144
N_CLUS = 256


def draw_samples(key, part):
    amplitude = 0.4
    leaf_key = jax.random.fold_in(key, 17)
    base_key = jax.random.fold_in(key, 29)
    log_scale = jax.random.uniform(leaf_key, (LEAVES, S), jnp.float32, -amplitude, amplitude)
    group_count = LEAVES // LEAVES_DEV
    tree_depth = group_count.bit_length() - 1
    for level_step in range(tree_depth):
        level_key = jax.random.fold_in(key, 100 + level_step)
        node_count = group_count >> level_step
        level_shift = jax.random.uniform(level_key, (node_count, S), jnp.float32, -amplitude, amplitude)
        log_scale = log_scale + jnp.repeat(level_shift, LEAVES_DEV << level_step, axis=0, total_repeat_length=LEAVES)
    base_values = jnp.clip(jax.random.normal(base_key, (LEAVES, LEAF, S), jnp.float32), -4.0, 4.0)
    scaled = base_values * jnp.exp(log_scale)[:, None, :]
    return jnp.clip(scaled, -8.0, 8.0).reshape(ROWS, S)


def block_scale(key, extent, split, low, largest):
    loudness, own = 1.0, jax.random.fold_in(key, 6)
    for dim, parts in split:
        heights = jnp.exp(jax.random.uniform(jax.random.fold_in(own, dim), (parts,), jnp.float32, low / len(split), largest / len(split)))
        loudness = loudness * jnp.repeat(heights, extent[dim] // parts).reshape([-1 if axis == dim else 1 for axis in range(len(extent))])
    return loudness


def scatter_about(own_key, dims, scale, limit, cuts=(), kind=jnp.bfloat16):
    drawn = jax.random.normal(own_key, dims, jnp.float32) * scale
    if len(cuts) > 0:
        drawn = block_scale(own_key, dims, cuts, -0.22, 0.18) * drawn
    return jnp.clip(drawn, min=-limit, max=limit).astype(kind)


def setup_inputs(seed: int = 0) -> dict:
    keys = jax.random.split(jax.random.key(seed), 4)
    samples = draw_samples(jax.random.fold_in(keys[3], 71), 0)
    sketch = scatter_about(keys[1], (S, K), S ** -0.5, 0.375, ((0, 2),), jnp.float32)
    leaf_slot = jax.vmap(lambda own: jax.random.permutation(own, LEAVES_DEV))(jax.random.split(keys[2], N_CLUS)).reshape((N_CLUS, LEAVES_DEV)).astype(jnp.int32)
    return dict(samples=samples, sketch=sketch, leaf_slot=leaf_slot)


highest = lax.Precision.HIGHEST

def factor(stacked):
    gram_matrix = jnp.einsum('mrk,mrl->mkl', stacked, stacked, precision=highest)
    width = gram_matrix.shape[1]
    identity = jnp.eye(width, dtype=jnp.float32)
    scale = jnp.einsum('mkk->m', gram_matrix)[:, None, None] + 1e-06
    start_root = gram_matrix / scale
    start_inverse = jnp.broadcast_to(identity, gram_matrix.shape).astype(jnp.float32)

    def newton_step(index, carry):
        root, inverse = carry
        middle = 1.5 * identity - 0.5 * jnp.einsum('mkl,mlj->mkj', inverse, root, precision=highest)
        return (jnp.einsum('mkl,mlj->mkj', root, middle, precision=highest), jnp.einsum('mkl,mlj->mkj', middle, inverse, precision=highest))
    root, inverse = lax.fori_loop(0, NS_STEPS, newton_step, (start_root, start_inverse))
    scale_root = jnp.sqrt(scale)
    orthonormal = jnp.einsum('mrk,mkl->mrl', stacked, inverse, precision=highest) / scale_root
    return (orthonormal, root * scale_root)

def reference(samples, sketch, leaf_slot):
    sketched = jnp.dot(samples, sketch, precision=highest).reshape(LEAVES, LEAF, K)
    leaf_basis, triangle = factor(sketched)
    offsets = jnp.arange(N_CLUS, dtype=jnp.int32)[:, None] * LEAVES_DEV
    order = (leaf_slot.astype(jnp.int32) + offsets).reshape(-1)
    factors = triangle[order]
    local_list = []
    for level_step in range(LEAVES_DEV.bit_length() - 1):
        transfer, factors = factor(factors.reshape(-1, 2 * K, K))
        local_list.append(transfer.reshape(N_CLUS, -1, 2 * K, K))
    if local_list:
        local_transfer = jnp.concatenate(local_list, axis=1).reshape(-1, 2 * K, K)
    else:
        local_transfer = jnp.zeros((0, 2 * K, K), jnp.float32)
    top_out = jnp.zeros((N_CLUS, 2 * K, K), jnp.float32)
    for level_step in range(1, N_CLUS.bit_length()):
        transfer, factors = factor(factors.reshape(-1, 2 * K, K))
        places = jnp.arange(N_CLUS >> level_step, dtype=jnp.int32) * 2 ** level_step + 2 ** (level_step - 1)
        top_out = top_out.at[places].set(transfer)
    return (leaf_basis.reshape(ROWS, K), local_transfer, top_out, factors[0])
```

```python
import jax
import jax.numpy as jnp
from jax import lax
from jax.sharding import PartitionSpec as P

NS_STEPS = 5
ROUND_BITS = 2


highest = lax.Precision.HIGHEST


def from_xor(block, axis, mask):
    count = lax.axis_size(axis)
    route = [(low, low ^ mask) for low in range(count) if low ^ mask < count]
    return lax.ppermute(block, axis, route)


def factor(stacked):
    gram_matrix = jnp.einsum("mrk,mrl->mkl", stacked, stacked, precision=highest)
    width = gram_matrix.shape[1]
    identity = jnp.eye(width, dtype=jnp.float32)
    scale = jnp.einsum("mkk->m", gram_matrix)[:, None, None] + 1e-06
    start_root = gram_matrix / scale
    start_inverse = jnp.broadcast_to(identity, gram_matrix.shape)

    def newton_step(index, carry):
        root, inverse = carry
        middle = 1.5 * identity - 0.5 * jnp.einsum("mkl,mlj->mkj", inverse, root, precision=highest)
        return (
            jnp.einsum("mkl,mlj->mkj", root, middle, precision=highest),
            jnp.einsum("mkl,mlj->mkj", middle, inverse, precision=highest),
        )

    root, inverse = lax.fori_loop(0, NS_STEPS, newton_step, (start_root, start_inverse))
    scale_root = jnp.sqrt(scale)
    orthonormal = jnp.einsum("mrk,mkl->mrl", stacked, inverse, precision=highest) / scale_root
    return (orthonormal, root * scale_root)


def body(samples, sketch, leaf_slot):
    columns = sketch.shape[1]
    leaf_count = leaf_slot.shape[1]
    partial_value = jnp.dot(samples, sketch, precision=highest).reshape(leaf_count, -1, columns)
    sketched = partial_value + from_xor(partial_value, "samp", 1)
    leaf_basis, triangle = factor(sketched)
    factors = triangle[leaf_slot[0]]
    local_list = []
    while factors.shape[0] > 1:
        stacked = factors.reshape(-1, 2 * columns, columns)
        transfer, factors = factor(stacked)
        local_list.append(transfer)
    local_transfer = jnp.concatenate(local_list, axis=0)
    position = lax.axis_index("clus")
    tree_depth = lax.axis_size("clus").bit_length() - 1
    top_out = jnp.zeros((1, 2 * columns, columns), jnp.float32)
    low_bit = 0
    while low_bit < tree_depth:
        width = min(ROUND_BITS, tree_depth - low_bit)
        members = 1 << width
        member = (position >> low_bit) & (members - 1)
        received = [factors] + [from_xor(factors, "clus", j << low_bit) for j in range(1, members)]
        received = jnp.concatenate(received, axis=0)
        slots = jnp.arange(members, dtype=jnp.int32) ^ member
        group = jnp.take(received, slots, axis=0)
        for level in range(width):
            stacked = group.reshape(-1, 2 * columns, columns)
            transfer, group = factor(stacked)
            level_bit = low_bit + level
            mine = lax.dynamic_index_in_dim(transfer, member >> (level + 1), 0, keepdims=True)
            owned = position % (2 << level_bit) == 1 << level_bit
            top_out = jnp.where(owned, mine, top_out)
        factors = group
        low_bit += width
    return (leaf_basis.reshape(-1, columns), local_transfer, top_out, factors[0])


def solution(mesh):
    return jax.shard_map(
        body,
        mesh=mesh,
        in_specs=(P("clus", "samp"), P("samp", None), P("clus", None)),
        out_specs=(P("clus", None), P("clus", None, None), P("clus", None, None), P()),
        check_vma=False,
    )
```

```python
import functools

import jax
import jax.numpy as jnp
from jax import lax
from jax.experimental import pallas as pl
from jax.experimental.pallas import tpu as pltpu
from jax.sharding import PartitionSpec as P

NS_STEPS = 5
ROUND_BITS = 2


highest = lax.Precision.HIGHEST


def from_xor(block, axis, mask):
    count = lax.axis_size(axis)
    route = [(low, low ^ mask) for low in range(count) if low ^ mask < count]
    return lax.ppermute(block, axis, route)


def mm(a, b):
    return jnp.dot(a, b, precision=highest, preferred_element_type=jnp.float32)


def gram(a):
    return lax.dot_general(a, a, (((0,), (0,)), ((), ())), precision=highest, preferred_element_type=jnp.float32)


def factor_nodes(nodes):
    width = nodes[0][0].shape[1]
    rows = lax.broadcasted_iota(jnp.int32, (width, width), 0)
    cols = lax.broadcasted_iota(jnp.int32, (width, width), 1)
    diag = rows == cols
    identity = jnp.where(diag, 1.0, 0.0).astype(jnp.float32)
    grams = []
    for parts in nodes:
        g = gram(parts[0])
        for part in parts[1:]:
            g = g + gram(part)
        grams.append(g)
    scales = [jnp.sum(jnp.where(diag, g, 0.0), keepdims=True) + 1e-06 for g in grams]
    roots = [g / c for g, c in zip(grams, scales)]
    inverses = [identity for _ in nodes]
    for _ in range(NS_STEPS):
        middles = [1.5 * identity - 0.5 * mm(w, y) for w, y in zip(inverses, roots)]
        roots, inverses = (
            [mm(y, m) for y, m in zip(roots, middles)],
            [mm(m, w) for m, w in zip(middles, inverses)],
        )
    results = []
    for parts, c, y, w in zip(nodes, scales, roots, inverses):
        s = jnp.sqrt(c)
        results.append(([mm(part, w) / s for part in parts], y * s))
    return results


def pair_levels(factors, levels, store):
    for level in range(levels):
        nodes = [[factors[2 * i], factors[2 * i + 1]] for i in range(len(factors) // 2)]
        results = factor_nodes(nodes)
        for i, (q_parts, _) in enumerate(results):
            store(level, i, q_parts)
        factors = [r for _, r in results]
    return factors


def local_kernel(slot_ref, z_ref, basis_ref, transfer_ref, top_ref):
    leaf_count = z_ref.shape[0]
    width = z_ref.shape[2]
    results = factor_nodes([[z_ref[i]] for i in range(leaf_count)])
    for i, (q_parts, _) in enumerate(results):
        basis_ref[i] = q_parts[0]
    triangles = [r for _, r in results]
    factors = []
    for j in range(leaf_count):
        pick = slot_ref[0, j]
        chosen = triangles[0]
        for i in range(1, leaf_count):
            chosen = jnp.where(pick == i, triangles[i], chosen)
        factors.append(chosen)
    offsets = []
    count = leaf_count
    total = 0
    while count > 1:
        count //= 2
        offsets.append(total)
        total += count

    def store(level, i, q_parts):
        for p, part in enumerate(q_parts):
            transfer_ref[offsets[level] + i, p * width:(p + 1) * width, :] = part

    factors = pair_levels(factors, len(offsets), store)
    top_ref[0] = factors[0]


def round_kernel(group_ref, *out_refs):
    members = group_ref.shape[0]
    width = group_ref.shape[2]
    levels = members.bit_length() - 1
    transfer_refs, top_ref = out_refs[:levels], out_refs[levels]

    def store(level, i, q_parts):
        for p, part in enumerate(q_parts):
            transfer_refs[level][i, p * width:(p + 1) * width, :] = part

    factors = pair_levels([group_ref[i] for i in range(members)], levels, store)
    top_ref[0] = factors[0]


def local_call(leaf_slot, sketched):
    leaf_count, rows, width = sketched.shape
    levels = leaf_count.bit_length() - 1
    vmem = pltpu.MemorySpace.VMEM
    return pl.pallas_call(
        local_kernel,
        out_shape=(
            jax.ShapeDtypeStruct((leaf_count, rows, width), jnp.float32),
            jax.ShapeDtypeStruct((leaf_count - 1, 2 * width, width), jnp.float32),
            jax.ShapeDtypeStruct((1, width, width), jnp.float32),
        ),
        in_specs=[pl.BlockSpec(memory_space=pltpu.MemorySpace.SMEM), pl.BlockSpec(memory_space=vmem)],
        out_specs=tuple(pl.BlockSpec(memory_space=vmem) for _ in range(3)),
    )(leaf_slot, sketched)


def round_call(group):
    members, width, _ = group.shape
    levels = members.bit_length() - 1
    vmem = pltpu.MemorySpace.VMEM
    shapes = [jax.ShapeDtypeStruct((members >> (level + 1), 2 * width, width), jnp.float32) for level in range(levels)]
    shapes.append(jax.ShapeDtypeStruct((1, width, width), jnp.float32))
    return pl.pallas_call(
        round_kernel,
        out_shape=tuple(shapes),
        in_specs=[pl.BlockSpec(memory_space=vmem)],
        out_specs=tuple(pl.BlockSpec(memory_space=vmem) for _ in shapes),
    )(group)


def body(samples, sketch, leaf_slot):
    columns = sketch.shape[1]
    leaf_count = leaf_slot.shape[1]
    partial_value = jnp.dot(samples, sketch, precision=highest).reshape(leaf_count, -1, columns)
    sketched = partial_value + from_xor(partial_value, "samp", 1)
    leaf_basis, local_transfer, factors = local_call(leaf_slot, sketched)
    position = lax.axis_index("clus")
    tree_depth = lax.axis_size("clus").bit_length() - 1
    top_out = jnp.zeros((1, 2 * columns, columns), jnp.float32)
    low_bit = 0
    while low_bit < tree_depth:
        width = min(ROUND_BITS, tree_depth - low_bit)
        members = 1 << width
        member = (position >> low_bit) & (members - 1)
        received = [factors] + [from_xor(factors, "clus", j << low_bit) for j in range(1, members)]
        received = jnp.concatenate(received, axis=0)
        slots = jnp.arange(members, dtype=jnp.int32) ^ member
        group = jnp.take(received, slots, axis=0)
        outs = round_call(group)
        for level in range(width):
            transfer = outs[level]
            level_bit = low_bit + level
            mine = lax.dynamic_index_in_dim(transfer, member >> (level + 1), 0, keepdims=True)
            owned = position % (2 << level_bit) == 1 << level_bit
            top_out = jnp.where(owned, mine, top_out)
        factors = outs[width]
        low_bit += width
    return (leaf_basis.reshape(-1, columns), local_transfer, top_out, factors[0])


def solution(mesh):
    return jax.shard_map(
        body,
        mesh=mesh,
        in_specs=(P("clus", "samp"), P("samp", None), P("clus", None)),
        out_specs=(P("clus", None), P("clus", None, None), P("clus", None, None), P()),
        check_vma=False,
    )
```

```python
import functools

import jax
import jax.numpy as jnp
from jax import lax
from jax.experimental import pallas as pl
from jax.experimental.pallas import tpu as pltpu
from jax.sharding import PartitionSpec as P

NS_STEPS = 5
ROUND_BITS = 2


highest = lax.Precision.HIGHEST


def from_xor(block, axis, mask):
    count = lax.axis_size(axis)
    route = [(low, low ^ mask) for low in range(count) if low ^ mask < count]
    return lax.ppermute(block, axis, route)


def mm(a, b):
    return jnp.dot(a, b, precision=highest, preferred_element_type=jnp.float32)


def gram(a):
    return lax.dot_general(a, a, (((0,), (0,)), ((), ())), precision=highest, preferred_element_type=jnp.float32)


def factor_nodes(nodes, keep_inverse=False):
    width = nodes[0][0].shape[1]
    rows = lax.broadcasted_iota(jnp.int32, (width, width), 0)
    cols = lax.broadcasted_iota(jnp.int32, (width, width), 1)
    diag = rows == cols
    identity = jnp.where(diag, 1.0, 0.0).astype(jnp.float32)
    grams = []
    for parts in nodes:
        g = gram(parts[0])
        for part in parts[1:]:
            g = g + gram(part)
        grams.append(g)
    scales = [jnp.sum(jnp.where(diag, g, 0.0), keepdims=True) + 1e-06 for g in grams]
    roots = [g / c for g, c in zip(grams, scales)]
    inverses = [identity for _ in nodes]
    for _ in range(NS_STEPS):
        middles = [1.5 * identity - 0.5 * mm(w, y) for w, y in zip(inverses, roots)]
        roots, inverses = (
            [mm(y, m) for y, m in zip(roots, middles)],
            [mm(m, w) for m, w in zip(middles, inverses)],
        )
    results = []
    for parts, c, y, w in zip(nodes, scales, roots, inverses):
        s = jnp.sqrt(c)
        if keep_inverse:
            results.append((w, y * s, s))
        else:
            results.append(([mm(part, w) / s for part in parts], y * s))
    return results


def pair_levels(factors, levels, store):
    for level in range(levels):
        nodes = [[factors[2 * i], factors[2 * i + 1]] for i in range(len(factors) // 2)]
        results = factor_nodes(nodes)
        for i, (q_parts, _) in enumerate(results):
            store(level, i, q_parts)
        factors = [r for _, r in results]
    return factors


def local_kernel(slot_ref, z_ref, other_ref, basis_ref, transfer_ref, top_ref):
    leaf_count = z_ref.shape[0]
    width = z_ref.shape[2]
    results = factor_nodes([[z_ref[i] + other_ref[i]] for i in range(leaf_count)])
    for i, (q_parts, _) in enumerate(results):
        basis_ref[i] = q_parts[0]
    triangles = [r for _, r in results]
    factors = []
    for j in range(leaf_count):
        pick = slot_ref[0, j]
        chosen = triangles[0]
        for i in range(1, leaf_count):
            chosen = jnp.where(pick == i, triangles[i], chosen)
        factors.append(chosen)
    offsets = []
    count = leaf_count
    total = 0
    while count > 1:
        count //= 2
        offsets.append(total)
        total += count

    def store(level, i, q_parts):
        for p, part in enumerate(q_parts):
            transfer_ref[offsets[level] + i, p * width:(p + 1) * width, :] = part

    factors = pair_levels(factors, len(offsets), store)
    top_ref[0] = factors[0]


def round_kernel(low_bit, own_ref, *refs):
    received_refs, top_in_ref, top_ref, next_ref = refs[:-3], refs[-3], refs[-2], refs[-1]
    width = own_ref.shape[2]
    levels = len(received_refs)
    members = 1 << levels
    position = lax.axis_index("clus")
    member = (position >> low_bit) & (members - 1)
    arrived = [own_ref[0]]
    for received_ref in received_refs:
        arrived += [received_ref[t] for t in range(received_ref.shape[0])]
    group = []
    for p in range(members):
        chosen = arrived[p]
        for t in range(members):
            if t != p:
                chosen = jnp.where(member == p ^ t, arrived[t], chosen)
        group.append(chosen)
    top = top_in_ref[0]
    factors = group
    for level in range(levels):
        nodes = [[factors[2 * i], factors[2 * i + 1]] for i in range(len(factors) // 2)]
        results = factor_nodes(nodes, keep_inverse=True)
        node = member >> (level + 1)
        mine_low, mine_high, mine_inverse, mine_scale = nodes[0][0], nodes[0][1], results[0][0], results[0][2]
        for i in range(1, len(nodes)):
            pick = node == i
            mine_low = jnp.where(pick, nodes[i][0], mine_low)
            mine_high = jnp.where(pick, nodes[i][1], mine_high)
            mine_inverse = jnp.where(pick, results[i][0], mine_inverse)
            mine_scale = jnp.where(pick, results[i][2], mine_scale)
        level_bit = low_bit + level
        owned = position % (2 << level_bit) == 1 << level_bit
        transfer = jnp.concatenate([mm(mine_low, mine_inverse) / mine_scale, mm(mine_high, mine_inverse) / mine_scale], axis=0)
        top = jnp.where(owned, transfer, top)
        factors = [r for _, r, _ in results]
    top_ref[0] = top
    next_ref[0] = factors[0]


def local_call(leaf_slot, partial_value, other_value):
    leaf_count, rows, width = partial_value.shape
    vmem = pltpu.MemorySpace.VMEM
    return pl.pallas_call(
        local_kernel,
        out_shape=(
            jax.ShapeDtypeStruct((leaf_count, rows, width), jnp.float32),
            jax.ShapeDtypeStruct((leaf_count - 1, 2 * width, width), jnp.float32),
            jax.ShapeDtypeStruct((1, width, width), jnp.float32),
        ),
        in_specs=[pl.BlockSpec(memory_space=pltpu.MemorySpace.SMEM), pl.BlockSpec(memory_space=vmem), pl.BlockSpec(memory_space=vmem)],
        out_specs=tuple(pl.BlockSpec(memory_space=vmem) for _ in range(3)),
    )(leaf_slot, partial_value, other_value)


def round_call(low_bit, own, received, top_in):
    width = own.shape[2]
    vmem = pltpu.MemorySpace.VMEM
    return pl.pallas_call(
        functools.partial(round_kernel, low_bit),
        out_shape=(
            jax.ShapeDtypeStruct(top_in.shape, jnp.float32),
            jax.ShapeDtypeStruct((1, width, width), jnp.float32),
        ),
        in_specs=[pl.BlockSpec(memory_space=vmem) for _ in range(len(received) + 2)],
        out_specs=(pl.BlockSpec(memory_space=vmem), pl.BlockSpec(memory_space=vmem)),
    )(own, *received, top_in)


def body(samples, sketch, leaf_slot):
    columns = sketch.shape[1]
    leaf_count = leaf_slot.shape[1]
    partial_value = jnp.dot(samples, sketch, precision=highest).reshape(leaf_count, -1, columns)
    other_value = from_xor(partial_value, "samp", 1)
    leaf_basis, local_transfer, factors = local_call(leaf_slot, partial_value, other_value)
    tree_depth = lax.axis_size("clus").bit_length() - 1
    top_out = jnp.zeros((1, 2 * columns, columns), jnp.float32)
    low_bit = 0
    while low_bit < tree_depth:
        width = min(ROUND_BITS, tree_depth - low_bit)
        gathered = factors
        received = []
        for step in range(width):
            arrived = from_xor(gathered, "clus", 1 << (low_bit + step))
            received.append(arrived)
            if step + 1 < width:
                gathered = jnp.concatenate([gathered, arrived], axis=0)
        top_out, factors = round_call(low_bit, factors, received, top_out)
        low_bit += width
    return (leaf_basis.reshape(-1, columns), local_transfer, top_out, factors[0])


def solution(mesh):
    return jax.shard_map(
        body,
        mesh=mesh,
        in_specs=(P("clus", "samp"), P("samp", None), P("clus", None)),
        out_specs=(P("clus", None), P("clus", None, None), P("clus", None, None), P()),
        check_vma=False,
    )
```

```python
import functools

import jax
import jax.numpy as jnp
from jax import lax
from jax.experimental import pallas as pl
from jax.experimental.pallas import tpu as pltpu
from jax.sharding import PartitionSpec as P

NS_STEPS = 5
ROUND_BITS = 2


highest = lax.Precision.HIGHEST


def from_xor(block, axis, mask):
    count = lax.axis_size(axis)
    route = [(low, low ^ mask) for low in range(count) if low ^ mask < count]
    return lax.ppermute(block, axis, route)


def mm(a, b):
    return jnp.dot(a, b, precision=highest, preferred_element_type=jnp.float32)


def gram(a):
    return lax.dot_general(a, a, (((0,), (0,)), ((), ())), precision=highest, preferred_element_type=jnp.float32)


def factor_nodes(nodes, keep_inverse=False):
    width = nodes[0][0].shape[1]
    rows = lax.broadcasted_iota(jnp.int32, (width, width), 0)
    cols = lax.broadcasted_iota(jnp.int32, (width, width), 1)
    diag = rows == cols
    identity = jnp.where(diag, 1.0, 0.0).astype(jnp.float32)
    grams = []
    for parts in nodes:
        g = gram(parts[0])
        for part in parts[1:]:
            g = g + gram(part)
        grams.append(g)
    scales = [jnp.sum(jnp.where(diag, g, 0.0), keepdims=True) + 1e-06 for g in grams]
    roots = [g / c for g, c in zip(grams, scales)]
    inverses = [identity for _ in nodes]
    for _ in range(NS_STEPS):
        middles = [1.5 * identity - 0.5 * mm(w, y) for w, y in zip(inverses, roots)]
        roots, inverses = (
            [mm(y, m) for y, m in zip(roots, middles)],
            [mm(m, w) for m, w in zip(middles, inverses)],
        )
    results = []
    for parts, c, y, w in zip(nodes, scales, roots, inverses):
        s = jnp.sqrt(c)
        if keep_inverse:
            results.append((w, y * s, s))
        else:
            results.append(([mm(part, w) / s for part in parts], y * s))
    return results


def pair_levels(factors, levels, store):
    for level in range(levels):
        nodes = [[factors[2 * i], factors[2 * i + 1]] for i in range(len(factors) // 2)]
        results = factor_nodes(nodes)
        for i, (q_parts, _) in enumerate(results):
            store(level, i, q_parts)
        factors = [r for _, r in results]
    return factors


def local_kernel(slot_ref, z_ref, other_ref, basis_ref, transfer_ref, top_ref):
    leaf_count = z_ref.shape[0]
    width = z_ref.shape[2]
    results = factor_nodes([[z_ref[i] + other_ref[i]] for i in range(leaf_count)])
    for i, (q_parts, _) in enumerate(results):
        basis_ref[i] = q_parts[0]
    triangles = [r for _, r in results]
    factors = []
    for j in range(leaf_count):
        pick = slot_ref[0, j]
        chosen = triangles[0]
        for i in range(1, leaf_count):
            chosen = jnp.where(pick == i, triangles[i], chosen)
        factors.append(chosen)
    offsets = []
    count = leaf_count
    total = 0
    while count > 1:
        count //= 2
        offsets.append(total)
        total += count

    def store(level, i, q_parts):
        for p, part in enumerate(q_parts):
            transfer_ref[offsets[level] + i, p * width:(p + 1) * width, :] = part

    factors = pair_levels(factors, len(offsets), store)
    top_ref[0] = factors[0]


def clus_position(axes):
    position = 0
    for name in axes:
        position = position * lax.axis_size(name) + lax.axis_index(name)
    return position


def round_kernel(low_bit, axes, group_ref, top_in_ref, top_ref, next_ref):
    members = group_ref.shape[0]
    levels = members.bit_length() - 1
    position = clus_position(axes)
    member = (position >> low_bit) & (members - 1)
    group = [group_ref[p] for p in range(members)]
    top = top_in_ref[0]
    factors = group
    for level in range(levels):
        nodes = [[factors[2 * i], factors[2 * i + 1]] for i in range(len(factors) // 2)]
        results = factor_nodes(nodes, keep_inverse=True)
        node = member >> (level + 1)
        mine_low, mine_high, mine_inverse, mine_scale = nodes[0][0], nodes[0][1], results[0][0], results[0][2]
        for i in range(1, len(nodes)):
            pick = node == i
            mine_low = jnp.where(pick, nodes[i][0], mine_low)
            mine_high = jnp.where(pick, nodes[i][1], mine_high)
            mine_inverse = jnp.where(pick, results[i][0], mine_inverse)
            mine_scale = jnp.where(pick, results[i][2], mine_scale)
        level_bit = low_bit + level
        owned = position % (2 << level_bit) == 1 << level_bit
        transfer = jnp.concatenate([mm(mine_low, mine_inverse) / mine_scale, mm(mine_high, mine_inverse) / mine_scale], axis=0)
        top = jnp.where(owned, transfer, top)
        factors = [r for _, r, _ in results]
    top_ref[0] = top
    next_ref[0] = factors[0]


def local_call(leaf_slot, partial_value, other_value):
    leaf_count, rows, width = partial_value.shape
    vmem = pltpu.MemorySpace.VMEM
    return pl.pallas_call(
        local_kernel,
        out_shape=(
            jax.ShapeDtypeStruct((leaf_count, rows, width), jnp.float32),
            jax.ShapeDtypeStruct((leaf_count - 1, 2 * width, width), jnp.float32),
            jax.ShapeDtypeStruct((1, width, width), jnp.float32),
        ),
        in_specs=[pl.BlockSpec(memory_space=pltpu.MemorySpace.SMEM), pl.BlockSpec(memory_space=vmem), pl.BlockSpec(memory_space=vmem)],
        out_specs=tuple(pl.BlockSpec(memory_space=vmem) for _ in range(3)),
    )(leaf_slot, partial_value, other_value)


def round_call(low_bit, axes, group, top_in):
    width = group.shape[2]
    vmem = pltpu.MemorySpace.VMEM
    return pl.pallas_call(
        functools.partial(round_kernel, low_bit, axes),
        out_shape=(
            jax.ShapeDtypeStruct(top_in.shape, jnp.float32),
            jax.ShapeDtypeStruct((1, width, width), jnp.float32),
        ),
        in_specs=[pl.BlockSpec(memory_space=vmem), pl.BlockSpec(memory_space=vmem)],
        out_specs=(pl.BlockSpec(memory_space=vmem), pl.BlockSpec(memory_space=vmem)),
    )(group, top_in)


def round_widths(count):
    depth = count.bit_length() - 1
    return [ROUND_BITS] * (depth // ROUND_BITS) + ([depth % ROUND_BITS] if depth % ROUND_BITS else [])


def body(axes, samples, sketch, leaf_slot):
    columns = sketch.shape[1]
    leaf_count = leaf_slot.shape[1]
    partial_value = jnp.dot(samples, sketch, precision=highest).reshape(leaf_count, -1, columns)
    other_value = from_xor(partial_value, "samp", 1)
    leaf_basis, local_transfer, factors = local_call(leaf_slot, partial_value, other_value)
    top_out = jnp.zeros((1, 2 * columns, columns), jnp.float32)
    low_bit = 0
    for name in reversed(axes):
        members = lax.axis_size(name)
        spread = jnp.broadcast_to(factors, (members,) + factors.shape[1:])
        group = lax.all_to_all(spread, name, 0, 0, tiled=True)
        top_out, factors = round_call(low_bit, axes, group, top_out)
        low_bit += members.bit_length() - 1
    return (leaf_basis.reshape(-1, columns), local_transfer, top_out, factors[0])


def solution(mesh):
    clus = mesh.shape["clus"]
    widths = round_widths(clus)
    axes = tuple(f"clus{i}" for i in range(len(widths)))
    sizes = tuple(1 << w for w in reversed(widths))
    devices = mesh.devices.reshape(sizes + (mesh.shape["samp"],))
    split = jax.sharding.Mesh(devices, axes + ("samp",))
    return jax.shard_map(
        functools.partial(body, axes),
        mesh=split,
        in_specs=(P(axes, "samp"), P("samp", None), P(axes, None)),
        out_specs=(P(axes, None), P(axes, None, None), P(axes, None, None), P()),
        check_vma=False,
    )
```

```python
import functools

import jax
import jax.numpy as jnp
from jax import lax
from jax.experimental import pallas as pl
from jax.experimental.pallas import tpu as pltpu
from jax.sharding import PartitionSpec as P

NS_STEPS = 5
ROUND_BITS = 2


highest = lax.Precision.HIGHEST


def from_xor(block, axis, mask):
    count = lax.axis_size(axis)
    route = [(low, low ^ mask) for low in range(count) if low ^ mask < count]
    return lax.ppermute(block, axis, route)


def mm(a, b):
    return jnp.dot(a, b, precision=highest, preferred_element_type=jnp.float32)


def gram(a):
    return lax.dot_general(a, a, (((0,), (0,)), ((), ())), precision=highest, preferred_element_type=jnp.float32)


def factor_nodes(nodes, keep_inverse=False):
    width = nodes[0][0].shape[1]
    rows = lax.broadcasted_iota(jnp.int32, (width, width), 0)
    cols = lax.broadcasted_iota(jnp.int32, (width, width), 1)
    diag = rows == cols
    identity = jnp.where(diag, 1.0, 0.0).astype(jnp.float32)
    grams = []
    for parts in nodes:
        g = gram(parts[0])
        for part in parts[1:]:
            g = g + gram(part)
        grams.append(g)
    scales = [jnp.sum(jnp.where(diag, g, 0.0), keepdims=True) + 1e-06 for g in grams]
    roots = [g / c for g, c in zip(grams, scales)]
    inverses = [identity for _ in nodes]
    for _ in range(NS_STEPS):
        middles = [1.5 * identity - 0.5 * mm(w, y) for w, y in zip(inverses, roots)]
        roots, inverses = (
            [mm(y, m) for y, m in zip(roots, middles)],
            [mm(m, w) for m, w in zip(middles, inverses)],
        )
    results = []
    for parts, c, y, w in zip(nodes, scales, roots, inverses):
        s = jnp.sqrt(c)
        if keep_inverse:
            results.append((w, y * s, s))
        else:
            results.append(([mm(part, w) / s for part in parts], y * s))
    return results


def pair_levels(factors, levels, store):
    for level in range(levels):
        nodes = [[factors[2 * i], factors[2 * i + 1]] for i in range(len(factors) // 2)]
        results = factor_nodes(nodes)
        for i, (q_parts, _) in enumerate(results):
            store(level, i, q_parts)
        factors = [r for _, r in results]
    return factors


def local_kernel(slot_ref, z_ref, other_ref, basis_ref, transfer_ref, top_ref):
    leaf_count = z_ref.shape[0]
    width = z_ref.shape[2]
    results = factor_nodes([[z_ref[i] + other_ref[i]] for i in range(leaf_count)])
    for i, (q_parts, _) in enumerate(results):
        basis_ref[i] = q_parts[0]
    triangles = [r for _, r in results]
    factors = []
    for j in range(leaf_count):
        pick = slot_ref[0, j]
        chosen = triangles[0]
        for i in range(1, leaf_count):
            chosen = jnp.where(pick == i, triangles[i], chosen)
        factors.append(chosen)
    offsets = []
    count = leaf_count
    total = 0
    while count > 1:
        count //= 2
        offsets.append(total)
        total += count

    def store(level, i, q_parts):
        for p, part in enumerate(q_parts):
            transfer_ref[offsets[level] + i, p * width:(p + 1) * width, :] = part

    factors = pair_levels(factors, len(offsets), store)
    for p in range(top_ref.shape[0]):
        top_ref[p] = factors[0]


def clus_position(axes):
    position = 0
    for name in axes:
        position = position * lax.axis_size(name) + lax.axis_index(name)
    return position


def round_kernel(low_bit, axes, group_ref, *refs):
    top_in_ref, top_ref, next_ref = refs if len(refs) == 3 else (None,) + refs
    members = group_ref.shape[0]
    levels = members.bit_length() - 1
    position = clus_position(axes)
    member = (position >> low_bit) & (members - 1)
    group = [group_ref[p] for p in range(members)]
    if top_in_ref is None:
        top = jnp.zeros(top_ref.shape[1:], jnp.float32)
    else:
        top = top_in_ref[0]
    factors = group
    for level in range(levels):
        nodes = [[factors[2 * i], factors[2 * i + 1]] for i in range(len(factors) // 2)]
        results = factor_nodes(nodes, keep_inverse=True)
        node = member >> (level + 1)
        mine_low, mine_high, mine_inverse, mine_scale = nodes[0][0], nodes[0][1], results[0][0], results[0][2]
        for i in range(1, len(nodes)):
            pick = node == i
            mine_low = jnp.where(pick, nodes[i][0], mine_low)
            mine_high = jnp.where(pick, nodes[i][1], mine_high)
            mine_inverse = jnp.where(pick, results[i][0], mine_inverse)
            mine_scale = jnp.where(pick, results[i][2], mine_scale)
        level_bit = low_bit + level
        owned = position % (2 << level_bit) == 1 << level_bit
        transfer = jnp.concatenate([mm(mine_low, mine_inverse) / mine_scale, mm(mine_high, mine_inverse) / mine_scale], axis=0)
        top = jnp.where(owned, transfer, top)
        factors = [r for _, r, _ in results]
    top_ref[0] = top
    for p in range(next_ref.shape[0]):
        next_ref[p] = factors[0]


def local_call(leaf_slot, partial_value, other_value, spread):
    leaf_count, rows, width = partial_value.shape
    vmem = pltpu.MemorySpace.VMEM
    return pl.pallas_call(
        local_kernel,
        out_shape=(
            jax.ShapeDtypeStruct((leaf_count, rows, width), jnp.float32),
            jax.ShapeDtypeStruct((leaf_count - 1, 2 * width, width), jnp.float32),
            jax.ShapeDtypeStruct((spread, width, width), jnp.float32),
        ),
        in_specs=[pl.BlockSpec(memory_space=pltpu.MemorySpace.SMEM), pl.BlockSpec(memory_space=vmem), pl.BlockSpec(memory_space=vmem)],
        out_specs=tuple(pl.BlockSpec(memory_space=vmem) for _ in range(3)),
    )(leaf_slot, partial_value, other_value)


def round_call(low_bit, axes, group, top_in, spread):
    width = group.shape[2]
    vmem = pltpu.MemorySpace.VMEM
    operands = [group] if top_in is None else [group, top_in]
    return pl.pallas_call(
        functools.partial(round_kernel, low_bit, axes),
        out_shape=(
            jax.ShapeDtypeStruct((1, 2 * width, width), jnp.float32),
            jax.ShapeDtypeStruct((spread, width, width), jnp.float32),
        ),
        in_specs=[pl.BlockSpec(memory_space=vmem) for _ in operands],
        out_specs=(pl.BlockSpec(memory_space=vmem), pl.BlockSpec(memory_space=vmem)),
    )(*operands)


def round_widths(count):
    depth = count.bit_length() - 1
    return [ROUND_BITS] * (depth // ROUND_BITS) + ([depth % ROUND_BITS] if depth % ROUND_BITS else [])


def body(axes, samples, sketch, leaf_slot):
    columns = sketch.shape[1]
    leaf_count = leaf_slot.shape[1]
    partial_value = jnp.dot(samples, sketch, precision=highest).reshape(leaf_count, -1, columns)
    other_value = from_xor(partial_value, "samp", 1)
    order = list(reversed(axes))
    sizes = [lax.axis_size(name) for name in order] + [1]
    leaf_basis, local_transfer, factors = local_call(leaf_slot, partial_value, other_value, sizes[0])
    top_out = None
    low_bit = 0
    for index, name in enumerate(order):
        group = lax.all_to_all(factors, name, 0, 0, tiled=True)
        top_out, factors = round_call(low_bit, axes, group, top_out, sizes[index + 1])
        low_bit += sizes[index].bit_length() - 1
    return (leaf_basis.reshape(-1, columns), local_transfer, top_out, factors[0])


def solution(mesh):
    clus = mesh.shape["clus"]
    widths = round_widths(clus)
    axes = tuple(f"clus{i}" for i in range(len(widths)))
    sizes = tuple(1 << w for w in reversed(widths))
    devices = mesh.devices.reshape(sizes + (mesh.shape["samp"],))
    split = jax.sharding.Mesh(devices, axes + ("samp",))
    return jax.shard_map(
        functools.partial(body, axes),
        mesh=split,
        in_specs=(P(axes, "samp"), P("samp", None), P(axes, None)),
        out_specs=(P(axes, None), P(axes, None, None), P(axes, None, None), P()),
        check_vma=False,
    )
```

```python
import functools

import jax
import jax.numpy as jnp
from jax import lax
from jax.experimental import pallas as pl
from jax.experimental.pallas import tpu as pltpu
from jax.sharding import PartitionSpec as P

NS_STEPS = 5
ROUND_BITS = 2


highest = lax.Precision.HIGHEST


def from_xor(block, axis, mask):
    count = lax.axis_size(axis)
    route = [(low, low ^ mask) for low in range(count) if low ^ mask < count]
    return lax.ppermute(block, axis, route)


def mm(a, b):
    return jnp.dot(a, b, precision=highest, preferred_element_type=jnp.float32)


def gram(a):
    return lax.dot_general(a, a, (((0,), (0,)), ((), ())), precision=highest, preferred_element_type=jnp.float32)


def factor_nodes(nodes, keep_inverse=False):
    width = nodes[0][0].shape[1]
    rows = lax.broadcasted_iota(jnp.int32, (width, width), 0)
    cols = lax.broadcasted_iota(jnp.int32, (width, width), 1)
    diag = rows == cols
    identity = jnp.where(diag, 1.0, 0.0).astype(jnp.float32)
    grams = []
    for parts in nodes:
        g = gram(parts[0])
        for part in parts[1:]:
            g = g + gram(part)
        grams.append(g)
    scales = []
    for parts in nodes:
        c = jnp.sum(parts[0] * parts[0], keepdims=True)
        for part in parts[1:]:
            c = c + jnp.sum(part * part, keepdims=True)
        scales.append(c + 1e-06)
    roots = [g * (1.0 / c) for g, c in zip(grams, scales)]
    middles = [1.5 * identity - 0.5 * y for y in roots]
    roots = [mm(y, m) for y, m in zip(roots, middles)]
    inverses = middles
    for _ in range(NS_STEPS - 1):
        middles = [1.5 * identity - 0.5 * mm(w, y) for w, y in zip(inverses, roots)]
        roots, inverses = (
            [mm(y, m) for y, m in zip(roots, middles)],
            [mm(m, w) for m, w in zip(middles, inverses)],
        )
    results = []
    for parts, c, y, w in zip(nodes, scales, roots, inverses):
        s = jnp.sqrt(c)
        if keep_inverse:
            results.append((w, y * s, s))
        else:
            results.append(([mm(part, w) / s for part in parts], y * s))
    return results


def pair_levels(factors, levels, store):
    for level in range(levels):
        nodes = [[factors[2 * i], factors[2 * i + 1]] for i in range(len(factors) // 2)]
        results = factor_nodes(nodes)
        for i, (q_parts, _) in enumerate(results):
            store(level, i, q_parts)
        factors = [r for _, r in results]
    return factors


def local_kernel(slot_ref, z_ref, other_ref, basis_ref, transfer_ref, top_ref):
    leaf_count = z_ref.shape[0]
    width = z_ref.shape[2]
    results = factor_nodes([[z_ref[i] + other_ref[i]] for i in range(leaf_count)])
    for i, (q_parts, _) in enumerate(results):
        basis_ref[i] = q_parts[0]
    triangles = [r for _, r in results]
    factors = []
    for j in range(leaf_count):
        pick = slot_ref[0, j]
        chosen = triangles[0]
        for i in range(1, leaf_count):
            chosen = jnp.where(pick == i, triangles[i], chosen)
        factors.append(chosen)
    offsets = []
    count = leaf_count
    total = 0
    while count > 1:
        count //= 2
        offsets.append(total)
        total += count

    def store(level, i, q_parts):
        for p, part in enumerate(q_parts):
            transfer_ref[offsets[level] + i, p * width:(p + 1) * width, :] = part

    factors = pair_levels(factors, len(offsets), store)
    for p in range(top_ref.shape[0]):
        top_ref[p] = factors[0]


def clus_position(axes):
    position = 0
    for name in axes:
        position = position * lax.axis_size(name) + lax.axis_index(name)
    return position


def round_kernel(low_bit, axes, group_ref, *refs):
    top_in_ref, top_ref, next_ref = refs if len(refs) == 3 else (None,) + refs
    members = group_ref.shape[0]
    levels = members.bit_length() - 1
    position = clus_position(axes)
    member = (position >> low_bit) & (members - 1)
    group = [group_ref[p] for p in range(members)]
    if top_in_ref is None:
        top = jnp.zeros(top_ref.shape[1:], jnp.float32)
    else:
        top = top_in_ref[0]
    factors = group
    for level in range(levels):
        nodes = [[factors[2 * i], factors[2 * i + 1]] for i in range(len(factors) // 2)]
        results = factor_nodes(nodes, keep_inverse=True)
        node = member >> (level + 1)
        mine_low, mine_high, mine_inverse, mine_scale = nodes[0][0], nodes[0][1], results[0][0], results[0][2]
        for i in range(1, len(nodes)):
            pick = node == i
            mine_low = jnp.where(pick, nodes[i][0], mine_low)
            mine_high = jnp.where(pick, nodes[i][1], mine_high)
            mine_inverse = jnp.where(pick, results[i][0], mine_inverse)
            mine_scale = jnp.where(pick, results[i][2], mine_scale)
        level_bit = low_bit + level
        owned = position % (2 << level_bit) == 1 << level_bit
        transfer = jnp.concatenate([mm(mine_low, mine_inverse) / mine_scale, mm(mine_high, mine_inverse) / mine_scale], axis=0)
        top = jnp.where(owned, transfer, top)
        factors = [r for _, r, _ in results]
    top_ref[0] = top
    for p in range(next_ref.shape[0]):
        next_ref[p] = factors[0]


def local_call(leaf_slot, partial_value, other_value, spread):
    leaf_count, rows, width = partial_value.shape
    vmem = pltpu.MemorySpace.VMEM
    return pl.pallas_call(
        local_kernel,
        out_shape=(
            jax.ShapeDtypeStruct((leaf_count, rows, width), jnp.float32),
            jax.ShapeDtypeStruct((leaf_count - 1, 2 * width, width), jnp.float32),
            jax.ShapeDtypeStruct((spread, width, width), jnp.float32),
        ),
        in_specs=[pl.BlockSpec(memory_space=pltpu.MemorySpace.SMEM), pl.BlockSpec(memory_space=vmem), pl.BlockSpec(memory_space=vmem)],
        out_specs=tuple(pl.BlockSpec(memory_space=vmem) for _ in range(3)),
    )(leaf_slot, partial_value, other_value)


def round_call(low_bit, axes, group, top_in, spread):
    width = group.shape[2]
    vmem = pltpu.MemorySpace.VMEM
    operands = [group] if top_in is None else [group, top_in]
    return pl.pallas_call(
        functools.partial(round_kernel, low_bit, axes),
        out_shape=(
            jax.ShapeDtypeStruct((1, 2 * width, width), jnp.float32),
            jax.ShapeDtypeStruct((spread, width, width), jnp.float32),
        ),
        in_specs=[pl.BlockSpec(memory_space=vmem) for _ in operands],
        out_specs=(pl.BlockSpec(memory_space=vmem), pl.BlockSpec(memory_space=vmem)),
    )(*operands)


def round_widths(count):
    depth = count.bit_length() - 1
    return [ROUND_BITS] * (depth // ROUND_BITS) + ([depth % ROUND_BITS] if depth % ROUND_BITS else [])


def body(axes, samples, sketch, leaf_slot):
    columns = sketch.shape[1]
    leaf_count = leaf_slot.shape[1]
    partial_value = jnp.dot(samples, sketch, precision=highest).reshape(leaf_count, -1, columns)
    other_value = from_xor(partial_value, "samp", 1)
    order = list(reversed(axes))
    sizes = [lax.axis_size(name) for name in order] + [1]
    leaf_basis, local_transfer, factors = local_call(leaf_slot, partial_value, other_value, sizes[0])
    top_out = None
    low_bit = 0
    for index, name in enumerate(order):
        group = lax.all_to_all(factors, name, 0, 0, tiled=True)
        top_out, factors = round_call(low_bit, axes, group, top_out, sizes[index + 1])
        low_bit += sizes[index].bit_length() - 1
    return (leaf_basis.reshape(-1, columns), local_transfer, top_out, factors[0])


def solution(mesh):
    clus = mesh.shape["clus"]
    widths = round_widths(clus)
    axes = tuple(f"clus{i}" for i in range(len(widths)))
    sizes = tuple(1 << w for w in reversed(widths))
    devices = mesh.devices.reshape(sizes + (mesh.shape["samp"],))
    split = jax.sharding.Mesh(devices, axes + ("samp",))
    return jax.shard_map(
        functools.partial(body, axes),
        mesh=split,
        in_specs=(P(axes, "samp"), P("samp", None), P(axes, None)),
        out_specs=(P(axes, None), P(axes, None, None), P(axes, None, None), P()),
        check_vma=False,
    )
```

```python
import functools

import jax
import jax.numpy as jnp
from jax import lax
from jax.experimental import pallas as pl
from jax.experimental.pallas import tpu as pltpu
from jax.sharding import PartitionSpec as P

NS_STEPS = 5
ROUND_BITS = 2


highest = lax.Precision.HIGHEST


def from_xor(block, axis, mask):
    count = lax.axis_size(axis)
    route = [(low, low ^ mask) for low in range(count) if low ^ mask < count]
    return lax.ppermute(block, axis, route)


def mm(a, b):
    a_high = a.astype(jnp.bfloat16)
    a_low = (a - a_high.astype(jnp.float32)).astype(jnp.bfloat16)
    b_high = b.astype(jnp.bfloat16)
    b_low = (b - b_high.astype(jnp.float32)).astype(jnp.bfloat16)
    dot = functools.partial(jnp.dot, preferred_element_type=jnp.float32)
    return dot(a_high, b_high) + (dot(a_high, b_low) + dot(a_low, b_high))


def gram(a):
    return lax.dot_general(a, a, (((0,), (0,)), ((), ())), precision=highest, preferred_element_type=jnp.float32)


def factor_nodes(nodes, keep_inverse=False):
    width = nodes[0][0].shape[1]
    rows = lax.broadcasted_iota(jnp.int32, (width, width), 0)
    cols = lax.broadcasted_iota(jnp.int32, (width, width), 1)
    diag = rows == cols
    identity = jnp.where(diag, 1.0, 0.0).astype(jnp.float32)
    grams = []
    for parts in nodes:
        g = gram(parts[0])
        for part in parts[1:]:
            g = g + gram(part)
        grams.append(g)
    scales = []
    for parts in nodes:
        c = jnp.sum(parts[0] * parts[0], keepdims=True)
        for part in parts[1:]:
            c = c + jnp.sum(part * part, keepdims=True)
        scales.append(c + 1e-06)
    roots = [g * (1.0 / c) for g, c in zip(grams, scales)]
    middles = [1.5 * identity - 0.5 * y for y in roots]
    roots = [mm(y, m) for y, m in zip(roots, middles)]
    inverses = middles
    for _ in range(NS_STEPS - 1):
        middles = [1.5 * identity - 0.5 * mm(w, y) for w, y in zip(inverses, roots)]
        roots, inverses = (
            [mm(y, m) for y, m in zip(roots, middles)],
            [mm(m, w) for m, w in zip(middles, inverses)],
        )
    results = []
    for parts, c, y, w in zip(nodes, scales, roots, inverses):
        s = jnp.sqrt(c)
        if keep_inverse:
            results.append((w, y * s, s))
        else:
            results.append(([mm(part, w) / s for part in parts], y * s))
    return results


def pair_levels(factors, levels, store):
    for level in range(levels):
        nodes = [[factors[2 * i], factors[2 * i + 1]] for i in range(len(factors) // 2)]
        results = factor_nodes(nodes)
        for i, (q_parts, _) in enumerate(results):
            store(level, i, q_parts)
        factors = [r for _, r in results]
    return factors


def local_kernel(slot_ref, z_ref, other_ref, basis_ref, transfer_ref, top_ref):
    leaf_count = z_ref.shape[0]
    width = z_ref.shape[2]
    results = factor_nodes([[z_ref[i] + other_ref[i]] for i in range(leaf_count)])
    for i, (q_parts, _) in enumerate(results):
        basis_ref[i] = q_parts[0]
    triangles = [r for _, r in results]
    factors = []
    for j in range(leaf_count):
        pick = slot_ref[0, j]
        chosen = triangles[0]
        for i in range(1, leaf_count):
            chosen = jnp.where(pick == i, triangles[i], chosen)
        factors.append(chosen)
    offsets = []
    count = leaf_count
    total = 0
    while count > 1:
        count //= 2
        offsets.append(total)
        total += count

    def store(level, i, q_parts):
        for p, part in enumerate(q_parts):
            transfer_ref[offsets[level] + i, p * width:(p + 1) * width, :] = part

    factors = pair_levels(factors, len(offsets), store)
    for p in range(top_ref.shape[0]):
        top_ref[p] = factors[0]


def clus_position(axes):
    position = 0
    for name in axes:
        position = position * lax.axis_size(name) + lax.axis_index(name)
    return position


def round_kernel(low_bit, axes, group_ref, *refs):
    top_in_ref, top_ref, next_ref = refs if len(refs) == 3 else (None,) + refs
    members = group_ref.shape[0]
    levels = members.bit_length() - 1
    position = clus_position(axes)
    member = (position >> low_bit) & (members - 1)
    group = [group_ref[p] for p in range(members)]
    if top_in_ref is None:
        top = jnp.zeros(top_ref.shape[1:], jnp.float32)
    else:
        top = top_in_ref[0]
    factors = group
    for level in range(levels):
        nodes = [[factors[2 * i], factors[2 * i + 1]] for i in range(len(factors) // 2)]
        results = factor_nodes(nodes, keep_inverse=True)
        node = member >> (level + 1)
        mine_low, mine_high, mine_inverse, mine_scale = nodes[0][0], nodes[0][1], results[0][0], results[0][2]
        for i in range(1, len(nodes)):
            pick = node == i
            mine_low = jnp.where(pick, nodes[i][0], mine_low)
            mine_high = jnp.where(pick, nodes[i][1], mine_high)
            mine_inverse = jnp.where(pick, results[i][0], mine_inverse)
            mine_scale = jnp.where(pick, results[i][2], mine_scale)
        level_bit = low_bit + level
        owned = position % (2 << level_bit) == 1 << level_bit
        transfer = jnp.concatenate([mm(mine_low, mine_inverse) / mine_scale, mm(mine_high, mine_inverse) / mine_scale], axis=0)
        top = jnp.where(owned, transfer, top)
        factors = [r for _, r, _ in results]
    top_ref[0] = top
    for p in range(next_ref.shape[0]):
        next_ref[p] = factors[0]


def local_call(leaf_slot, partial_value, other_value, spread):
    leaf_count, rows, width = partial_value.shape
    vmem = pltpu.MemorySpace.VMEM
    return pl.pallas_call(
        local_kernel,
        out_shape=(
            jax.ShapeDtypeStruct((leaf_count, rows, width), jnp.float32),
            jax.ShapeDtypeStruct((leaf_count - 1, 2 * width, width), jnp.float32),
            jax.ShapeDtypeStruct((spread, width, width), jnp.float32),
        ),
        in_specs=[pl.BlockSpec(memory_space=pltpu.MemorySpace.SMEM), pl.BlockSpec(memory_space=vmem), pl.BlockSpec(memory_space=vmem)],
        out_specs=tuple(pl.BlockSpec(memory_space=vmem) for _ in range(3)),
    )(leaf_slot, partial_value, other_value)


def round_call(low_bit, axes, group, top_in, spread):
    width = group.shape[2]
    vmem = pltpu.MemorySpace.VMEM
    operands = [group] if top_in is None else [group, top_in]
    return pl.pallas_call(
        functools.partial(round_kernel, low_bit, axes),
        out_shape=(
            jax.ShapeDtypeStruct((1, 2 * width, width), jnp.float32),
            jax.ShapeDtypeStruct((spread, width, width), jnp.float32),
        ),
        in_specs=[pl.BlockSpec(memory_space=vmem) for _ in operands],
        out_specs=(pl.BlockSpec(memory_space=vmem), pl.BlockSpec(memory_space=vmem)),
    )(*operands)


def round_widths(count):
    depth = count.bit_length() - 1
    return [ROUND_BITS] * (depth // ROUND_BITS) + ([depth % ROUND_BITS] if depth % ROUND_BITS else [])


def body(axes, samples, sketch, leaf_slot):
    columns = sketch.shape[1]
    leaf_count = leaf_slot.shape[1]
    partial_value = jnp.dot(samples, sketch, precision=highest).reshape(leaf_count, -1, columns)
    other_value = from_xor(partial_value, "samp", 1)
    order = list(reversed(axes))
    sizes = [lax.axis_size(name) for name in order] + [1]
    leaf_basis, local_transfer, factors = local_call(leaf_slot, partial_value, other_value, sizes[0])
    top_out = None
    low_bit = 0
    for index, name in enumerate(order):
        group = lax.all_to_all(factors, name, 0, 0, tiled=True)
        top_out, factors = round_call(low_bit, axes, group, top_out, sizes[index + 1])
        low_bit += sizes[index].bit_length() - 1
    return (leaf_basis.reshape(-1, columns), local_transfer, top_out, factors[0])


def solution(mesh):
    clus = mesh.shape["clus"]
    widths = round_widths(clus)
    axes = tuple(f"clus{i}" for i in range(len(widths)))
    sizes = tuple(1 << w for w in reversed(widths))
    devices = mesh.devices.reshape(sizes + (mesh.shape["samp"],))
    split = jax.sharding.Mesh(devices, axes + ("samp",))
    return jax.shard_map(
        functools.partial(body, axes),
        mesh=split,
        in_specs=(P(axes, "samp"), P("samp", None), P(axes, None)),
        out_specs=(P(axes, None), P(axes, None, None), P(axes, None, None), P()),
        check_vma=False,
    )
```

```python
import functools

import jax
import jax.numpy as jnp
from jax import lax
from jax.experimental import pallas as pl
from jax.experimental.pallas import tpu as pltpu
from jax.sharding import PartitionSpec as P

NS_STEPS = 5
ROUND_BITS = 3


highest = lax.Precision.HIGHEST


def from_xor(block, axis, mask):
    count = lax.axis_size(axis)
    route = [(low, low ^ mask) for low in range(count) if low ^ mask < count]
    return lax.ppermute(block, axis, route)


def mm(a, b):
    a_high = a.astype(jnp.bfloat16)
    a_low = (a - a_high.astype(jnp.float32)).astype(jnp.bfloat16)
    b_high = b.astype(jnp.bfloat16)
    b_low = (b - b_high.astype(jnp.float32)).astype(jnp.bfloat16)
    dot = functools.partial(jnp.dot, preferred_element_type=jnp.float32)
    return dot(a_high, b_high) + (dot(a_high, b_low) + dot(a_low, b_high))


def gram(a):
    return lax.dot_general(a, a, (((0,), (0,)), ((), ())), precision=highest, preferred_element_type=jnp.float32)


def factor_nodes(nodes, keep_inverse=False):
    width = nodes[0][0].shape[1]
    rows = lax.broadcasted_iota(jnp.int32, (width, width), 0)
    cols = lax.broadcasted_iota(jnp.int32, (width, width), 1)
    diag = rows == cols
    identity = jnp.where(diag, 1.0, 0.0).astype(jnp.float32)
    grams = []
    for parts in nodes:
        g = gram(parts[0])
        for part in parts[1:]:
            g = g + gram(part)
        grams.append(g)
    scales = []
    for parts in nodes:
        c = jnp.sum(parts[0] * parts[0], keepdims=True)
        for part in parts[1:]:
            c = c + jnp.sum(part * part, keepdims=True)
        scales.append(c + 1e-06)
    roots = [g * (1.0 / c) for g, c in zip(grams, scales)]
    middles = [1.5 * identity - 0.5 * y for y in roots]
    roots = [mm(y, m) for y, m in zip(roots, middles)]
    inverses = middles
    for _ in range(NS_STEPS - 1):
        middles = [1.5 * identity - 0.5 * mm(w, y) for w, y in zip(inverses, roots)]
        roots, inverses = (
            [mm(y, m) for y, m in zip(roots, middles)],
            [mm(m, w) for m, w in zip(middles, inverses)],
        )
    results = []
    for parts, c, y, w in zip(nodes, scales, roots, inverses):
        s = jnp.sqrt(c)
        if keep_inverse:
            results.append((w, y * s, s))
        else:
            results.append(([mm(part, w) / s for part in parts], y * s))
    return results


def pair_levels(factors, levels, store):
    for level in range(levels):
        nodes = [[factors[2 * i], factors[2 * i + 1]] for i in range(len(factors) // 2)]
        results = factor_nodes(nodes)
        for i, (q_parts, _) in enumerate(results):
            store(level, i, q_parts)
        factors = [r for _, r in results]
    return factors


def local_kernel(slot_ref, z_ref, other_ref, basis_ref, transfer_ref, top_ref):
    leaf_count = z_ref.shape[0]
    width = z_ref.shape[2]
    results = factor_nodes([[z_ref[i] + other_ref[i]] for i in range(leaf_count)])
    for i, (q_parts, _) in enumerate(results):
        basis_ref[i] = q_parts[0]
    triangles = [r for _, r in results]
    factors = []
    for j in range(leaf_count):
        pick = slot_ref[0, j]
        chosen = triangles[0]
        for i in range(1, leaf_count):
            chosen = jnp.where(pick == i, triangles[i], chosen)
        factors.append(chosen)
    offsets = []
    count = leaf_count
    total = 0
    while count > 1:
        count //= 2
        offsets.append(total)
        total += count

    def store(level, i, q_parts):
        for p, part in enumerate(q_parts):
            transfer_ref[offsets[level] + i, p * width:(p + 1) * width, :] = part

    factors = pair_levels(factors, len(offsets), store)
    for p in range(top_ref.shape[0]):
        top_ref[p] = factors[0]


def clus_position(axes):
    position = 0
    for name in axes:
        position = position * lax.axis_size(name) + lax.axis_index(name)
    return position


def round_kernel(low_bit, axes, group_ref, *refs):
    top_in_ref, top_ref, next_ref = refs if len(refs) == 3 else (None,) + refs
    members = group_ref.shape[0]
    levels = members.bit_length() - 1
    position = clus_position(axes)
    member = (position >> low_bit) & (members - 1)
    group = [group_ref[p] for p in range(members)]
    if top_in_ref is None:
        top = jnp.zeros(top_ref.shape[1:], jnp.float32)
    else:
        top = top_in_ref[0]
    factors = group
    for level in range(levels):
        nodes = [[factors[2 * i], factors[2 * i + 1]] for i in range(len(factors) // 2)]
        results = factor_nodes(nodes, keep_inverse=True)
        node = member >> (level + 1)
        mine_low, mine_high, mine_inverse, mine_scale = nodes[0][0], nodes[0][1], results[0][0], results[0][2]
        for i in range(1, len(nodes)):
            pick = node == i
            mine_low = jnp.where(pick, nodes[i][0], mine_low)
            mine_high = jnp.where(pick, nodes[i][1], mine_high)
            mine_inverse = jnp.where(pick, results[i][0], mine_inverse)
            mine_scale = jnp.where(pick, results[i][2], mine_scale)
        level_bit = low_bit + level
        owned = position % (2 << level_bit) == 1 << level_bit
        transfer = jnp.concatenate([mm(mine_low, mine_inverse) / mine_scale, mm(mine_high, mine_inverse) / mine_scale], axis=0)
        top = jnp.where(owned, transfer, top)
        factors = [r for _, r, _ in results]
    top_ref[0] = top
    for p in range(next_ref.shape[0]):
        next_ref[p] = factors[0]


def local_call(leaf_slot, partial_value, other_value, spread):
    leaf_count, rows, width = partial_value.shape
    vmem = pltpu.MemorySpace.VMEM
    return pl.pallas_call(
        local_kernel,
        out_shape=(
            jax.ShapeDtypeStruct((leaf_count, rows, width), jnp.float32),
            jax.ShapeDtypeStruct((leaf_count - 1, 2 * width, width), jnp.float32),
            jax.ShapeDtypeStruct((spread, width, width), jnp.float32),
        ),
        in_specs=[pl.BlockSpec(memory_space=pltpu.MemorySpace.SMEM), pl.BlockSpec(memory_space=vmem), pl.BlockSpec(memory_space=vmem)],
        out_specs=tuple(pl.BlockSpec(memory_space=vmem) for _ in range(3)),
    )(leaf_slot, partial_value, other_value)


def round_call(low_bit, axes, group, top_in, spread):
    width = group.shape[2]
    vmem = pltpu.MemorySpace.VMEM
    operands = [group] if top_in is None else [group, top_in]
    return pl.pallas_call(
        functools.partial(round_kernel, low_bit, axes),
        out_shape=(
            jax.ShapeDtypeStruct((1, 2 * width, width), jnp.float32),
            jax.ShapeDtypeStruct((spread, width, width), jnp.float32),
        ),
        in_specs=[pl.BlockSpec(memory_space=vmem) for _ in operands],
        out_specs=(pl.BlockSpec(memory_space=vmem), pl.BlockSpec(memory_space=vmem)),
    )(*operands)


def round_widths(count):
    depth = count.bit_length() - 1
    return [ROUND_BITS] * (depth // ROUND_BITS) + ([depth % ROUND_BITS] if depth % ROUND_BITS else [])


def body(axes, samples, sketch, leaf_slot):
    columns = sketch.shape[1]
    leaf_count = leaf_slot.shape[1]
    partial_value = jnp.dot(samples, sketch, precision=highest).reshape(leaf_count, -1, columns)
    other_value = from_xor(partial_value, "samp", 1)
    order = list(reversed(axes))
    sizes = [lax.axis_size(name) for name in order] + [1]
    leaf_basis, local_transfer, factors = local_call(leaf_slot, partial_value, other_value, sizes[0])
    top_out = None
    low_bit = 0
    for index, name in enumerate(order):
        group = lax.all_to_all(factors, name, 0, 0, tiled=True)
        top_out, factors = round_call(low_bit, axes, group, top_out, sizes[index + 1])
        low_bit += sizes[index].bit_length() - 1
    return (leaf_basis.reshape(-1, columns), local_transfer, top_out, factors[0])


def solution(mesh):
    clus = mesh.shape["clus"]
    widths = round_widths(clus)
    axes = tuple(f"clus{i}" for i in range(len(widths)))
    sizes = tuple(1 << w for w in reversed(widths))
    devices = mesh.devices.reshape(sizes + (mesh.shape["samp"],))
    split = jax.sharding.Mesh(devices, axes + ("samp",))
    return jax.shard_map(
        functools.partial(body, axes),
        mesh=split,
        in_specs=(P(axes, "samp"), P("samp", None), P(axes, None)),
        out_specs=(P(axes, None), P(axes, None, None), P(axes, None, None), P()),
        check_vma=False,
    )
```

```python
import functools

import jax
import jax.numpy as jnp
from jax import lax
from jax.experimental import pallas as pl
from jax.experimental.pallas import tpu as pltpu
from jax.sharding import PartitionSpec as P

NS_STEPS = 5
ROUND_BITS = 3


highest = lax.Precision.HIGHEST


def from_xor(block, axis, mask):
    count = lax.axis_size(axis)
    route = [(low, low ^ mask) for low in range(count) if low ^ mask < count]
    return lax.ppermute(block, axis, route)


def mm(a, b):
    a_high = a.astype(jnp.bfloat16)
    a_low = (a - a_high.astype(jnp.float32)).astype(jnp.bfloat16)
    b_high = b.astype(jnp.bfloat16)
    b_low = (b - b_high.astype(jnp.float32)).astype(jnp.bfloat16)
    dot = functools.partial(jnp.dot, preferred_element_type=jnp.float32)
    return dot(a_high, b_high) + (dot(a_high, b_low) + dot(a_low, b_high))


def gram(a):
    high = a.astype(jnp.bfloat16)
    low = (a - high.astype(jnp.float32)).astype(jnp.bfloat16)
    dims = (((0,), (0,)), ((), ()))
    dot = functools.partial(lax.dot_general, dimension_numbers=dims, preferred_element_type=jnp.float32)
    return dot(high, high) + (dot(high, low) + dot(low, high))


def factor_nodes(nodes, keep_inverse=False):
    width = nodes[0][0].shape[1]
    rows = lax.broadcasted_iota(jnp.int32, (width, width), 0)
    cols = lax.broadcasted_iota(jnp.int32, (width, width), 1)
    diag = rows == cols
    identity = jnp.where(diag, 1.0, 0.0).astype(jnp.float32)
    grams = []
    for parts in nodes:
        g = gram(parts[0])
        for part in parts[1:]:
            g = g + gram(part)
        grams.append(g)
    scales = []
    for parts in nodes:
        c = jnp.sum(parts[0] * parts[0], keepdims=True)
        for part in parts[1:]:
            c = c + jnp.sum(part * part, keepdims=True)
        scales.append(c + 1e-06)
    roots = [g * (1.0 / c) for g, c in zip(grams, scales)]
    middles = [1.5 * identity - 0.5 * y for y in roots]
    roots = [mm(y, m) for y, m in zip(roots, middles)]
    inverses = middles
    for _ in range(NS_STEPS - 1):
        middles = [1.5 * identity - 0.5 * mm(w, y) for w, y in zip(inverses, roots)]
        roots, inverses = (
            [mm(y, m) for y, m in zip(roots, middles)],
            [mm(m, w) for m, w in zip(middles, inverses)],
        )
    results = []
    for parts, c, y, w in zip(nodes, scales, roots, inverses):
        s = jnp.sqrt(c)
        if keep_inverse:
            results.append((w, y * s, s))
        else:
            results.append(([mm(part, w) / s for part in parts], y * s))
    return results


def pair_levels(factors, levels, store):
    for level in range(levels):
        nodes = [[factors[2 * i], factors[2 * i + 1]] for i in range(len(factors) // 2)]
        results = factor_nodes(nodes)
        for i, (q_parts, _) in enumerate(results):
            store(level, i, q_parts)
        factors = [r for _, r in results]
    return factors


def local_kernel(slot_ref, z_ref, other_ref, basis_ref, transfer_ref, top_ref):
    leaf_count = z_ref.shape[0]
    width = z_ref.shape[2]
    results = factor_nodes([[z_ref[i] + other_ref[i]] for i in range(leaf_count)])
    for i, (q_parts, _) in enumerate(results):
        basis_ref[i] = q_parts[0]
    triangles = [r for _, r in results]
    factors = []
    for j in range(leaf_count):
        pick = slot_ref[0, j]
        chosen = triangles[0]
        for i in range(1, leaf_count):
            chosen = jnp.where(pick == i, triangles[i], chosen)
        factors.append(chosen)
    offsets = []
    count = leaf_count
    total = 0
    while count > 1:
        count //= 2
        offsets.append(total)
        total += count

    def store(level, i, q_parts):
        for p, part in enumerate(q_parts):
            transfer_ref[offsets[level] + i, p * width:(p + 1) * width, :] = part

    factors = pair_levels(factors, len(offsets), store)
    for p in range(top_ref.shape[0]):
        top_ref[p] = factors[0]


def clus_position(axes):
    position = 0
    for name in axes:
        position = position * lax.axis_size(name) + lax.axis_index(name)
    return position


def round_kernel(low_bit, axes, group_ref, *refs):
    top_in_ref, top_ref, next_ref = refs if len(refs) == 3 else (None,) + refs
    members = group_ref.shape[0]
    levels = members.bit_length() - 1
    position = clus_position(axes)
    member = (position >> low_bit) & (members - 1)
    group = [group_ref[p] for p in range(members)]
    if top_in_ref is None:
        top = jnp.zeros(top_ref.shape[1:], jnp.float32)
    else:
        top = top_in_ref[0]
    factors = group
    for level in range(levels):
        nodes = [[factors[2 * i], factors[2 * i + 1]] for i in range(len(factors) // 2)]
        results = factor_nodes(nodes, keep_inverse=True)
        node = member >> (level + 1)
        mine_low, mine_high, mine_inverse, mine_scale = nodes[0][0], nodes[0][1], results[0][0], results[0][2]
        for i in range(1, len(nodes)):
            pick = node == i
            mine_low = jnp.where(pick, nodes[i][0], mine_low)
            mine_high = jnp.where(pick, nodes[i][1], mine_high)
            mine_inverse = jnp.where(pick, results[i][0], mine_inverse)
            mine_scale = jnp.where(pick, results[i][2], mine_scale)
        level_bit = low_bit + level
        owned = position % (2 << level_bit) == 1 << level_bit
        transfer = jnp.concatenate([mm(mine_low, mine_inverse) / mine_scale, mm(mine_high, mine_inverse) / mine_scale], axis=0)
        top = jnp.where(owned, transfer, top)
        factors = [r for _, r, _ in results]
    top_ref[0] = top
    for p in range(next_ref.shape[0]):
        next_ref[p] = factors[0]


def local_call(leaf_slot, partial_value, other_value, spread):
    leaf_count, rows, width = partial_value.shape
    vmem = pltpu.MemorySpace.VMEM
    return pl.pallas_call(
        local_kernel,
        out_shape=(
            jax.ShapeDtypeStruct((leaf_count, rows, width), jnp.float32),
            jax.ShapeDtypeStruct((leaf_count - 1, 2 * width, width), jnp.float32),
            jax.ShapeDtypeStruct((spread, width, width), jnp.float32),
        ),
        in_specs=[pl.BlockSpec(memory_space=pltpu.MemorySpace.SMEM), pl.BlockSpec(memory_space=vmem), pl.BlockSpec(memory_space=vmem)],
        out_specs=tuple(pl.BlockSpec(memory_space=vmem) for _ in range(3)),
    )(leaf_slot, partial_value, other_value)


def round_call(low_bit, axes, group, top_in, spread):
    width = group.shape[2]
    vmem = pltpu.MemorySpace.VMEM
    operands = [group] if top_in is None else [group, top_in]
    return pl.pallas_call(
        functools.partial(round_kernel, low_bit, axes),
        out_shape=(
            jax.ShapeDtypeStruct((1, 2 * width, width), jnp.float32),
            jax.ShapeDtypeStruct((spread, width, width), jnp.float32),
        ),
        in_specs=[pl.BlockSpec(memory_space=vmem) for _ in operands],
        out_specs=(pl.BlockSpec(memory_space=vmem), pl.BlockSpec(memory_space=vmem)),
    )(*operands)


def round_widths(count):
    depth = count.bit_length() - 1
    return [ROUND_BITS] * (depth // ROUND_BITS) + ([depth % ROUND_BITS] if depth % ROUND_BITS else [])


def body(axes, samples, sketch, leaf_slot):
    columns = sketch.shape[1]
    leaf_count = leaf_slot.shape[1]
    partial_value = jnp.dot(samples, sketch, precision=highest).reshape(leaf_count, -1, columns)
    other_value = from_xor(partial_value, "samp", 1)
    order = list(reversed(axes))
    sizes = [lax.axis_size(name) for name in order] + [1]
    leaf_basis, local_transfer, factors = local_call(leaf_slot, partial_value, other_value, sizes[0])
    top_out = None
    low_bit = 0
    for index, name in enumerate(order):
        group = lax.all_to_all(factors, name, 0, 0, tiled=True)
        top_out, factors = round_call(low_bit, axes, group, top_out, sizes[index + 1])
        low_bit += sizes[index].bit_length() - 1
    return (leaf_basis.reshape(-1, columns), local_transfer, top_out, factors[0])


def solution(mesh):
    clus = mesh.shape["clus"]
    widths = round_widths(clus)
    axes = tuple(f"clus{i}" for i in range(len(widths)))
    sizes = tuple(1 << w for w in reversed(widths))
    devices = mesh.devices.reshape(sizes + (mesh.shape["samp"],))
    split = jax.sharding.Mesh(devices, axes + ("samp",))
    return jax.shard_map(
        functools.partial(body, axes),
        mesh=split,
        in_specs=(P(axes, "samp"), P("samp", None), P(axes, None)),
        out_specs=(P(axes, None), P(axes, None, None), P(axes, None, None), P()),
        check_vma=False,
    )
```

```python
import functools

import jax
import jax.numpy as jnp
from jax import lax
from jax.experimental import pallas as pl
from jax.experimental.pallas import tpu as pltpu
from jax.sharding import PartitionSpec as P

NS_STEPS = 5
ROUND_BITS = 3


highest = lax.Precision.HIGHEST


def from_xor(block, axis, mask):
    count = lax.axis_size(axis)
    route = [(low, low ^ mask) for low in range(count) if low ^ mask < count]
    return lax.ppermute(block, axis, route)


def mm(a, b):
    a_high = a.astype(jnp.bfloat16)
    a_low = (a - a_high.astype(jnp.float32)).astype(jnp.bfloat16)
    b_high = b.astype(jnp.bfloat16)
    b_low = (b - b_high.astype(jnp.float32)).astype(jnp.bfloat16)
    dot = functools.partial(jnp.dot, preferred_element_type=jnp.float32)
    return dot(a_high, b_high) + (dot(a_high, b_low) + dot(a_low, b_high))


def gram(a):
    high = a.astype(jnp.bfloat16)
    low = (a - high.astype(jnp.float32)).astype(jnp.bfloat16)
    dims = (((0,), (0,)), ((), ()))
    dot = functools.partial(lax.dot_general, dimension_numbers=dims, preferred_element_type=jnp.float32)
    return dot(high, high) + (dot(high, low) + dot(low, high))


def factor_nodes(nodes, keep_inverse=False):
    width = nodes[0][0].shape[1]
    rows = lax.broadcasted_iota(jnp.int32, (width, width), 0)
    cols = lax.broadcasted_iota(jnp.int32, (width, width), 1)
    diag = rows == cols
    identity = jnp.where(diag, 1.0, 0.0).astype(jnp.float32)
    grams = []
    for parts in nodes:
        g = gram(parts[0])
        for part in parts[1:]:
            g = g + gram(part)
        grams.append(g)
    scales = []
    for parts in nodes:
        c = jnp.sum(parts[0] * parts[0], keepdims=True)
        for part in parts[1:]:
            c = c + jnp.sum(part * part, keepdims=True)
        scales.append(c + 1e-06)
    roots = [g * (1.0 / c) for g, c in zip(grams, scales)]
    middles = [1.5 * identity - 0.5 * y for y in roots]
    roots = [mm(y, m) for y, m in zip(roots, middles)]
    inverses = middles
    for _ in range(NS_STEPS - 1):
        middles = [1.5 * identity - 0.5 * mm(w, y) for w, y in zip(inverses, roots)]
        roots, inverses = (
            [mm(y, m) for y, m in zip(roots, middles)],
            [mm(m, w) for m, w in zip(middles, inverses)],
        )
    results = []
    for parts, c, y, w in zip(nodes, scales, roots, inverses):
        s = jnp.sqrt(c)
        if keep_inverse:
            results.append((w, y * s, s))
        else:
            results.append(([mm(part, w) / s for part in parts], y * s))
    return results


def pair_levels(factors, levels, store):
    for level in range(levels):
        nodes = [[factors[2 * i], factors[2 * i + 1]] for i in range(len(factors) // 2)]
        results = factor_nodes(nodes)
        for i, (q_parts, _) in enumerate(results):
            store(level, i, q_parts)
        factors = [r for _, r in results]
    return factors


def local_kernel(slot_ref, z_ref, other_ref, basis_ref, transfer_ref, top_ref):
    leaf_count = z_ref.shape[0]
    width = z_ref.shape[2]
    results = factor_nodes([[z_ref[i] + other_ref[i]] for i in range(leaf_count)])
    for i, (q_parts, _) in enumerate(results):
        basis_ref[i] = q_parts[0]
    triangles = [r for _, r in results]
    factors = []
    for j in range(leaf_count):
        pick = slot_ref[0, j]
        chosen = triangles[0]
        for i in range(1, leaf_count):
            chosen = jnp.where(pick == i, triangles[i], chosen)
        factors.append(chosen)
    offsets = []
    count = leaf_count
    total = 0
    while count > 1:
        count //= 2
        offsets.append(total)
        total += count

    def store(level, i, q_parts):
        for p, part in enumerate(q_parts):
            transfer_ref[offsets[level] + i, p * width:(p + 1) * width, :] = part

    factors = pair_levels(factors, len(offsets), store)
    for p in range(top_ref.shape[0]):
        top_ref[p] = factors[0]


def clus_position(axes):
    position = 0
    for name in axes:
        position = position * lax.axis_size(name) + lax.axis_index(name)
    return position


def round_kernel(low_bit, axes, group_ref, *refs):
    top_in_ref, top_ref, next_ref = refs if len(refs) == 3 else (None,) + refs
    members = group_ref.shape[0]
    levels = members.bit_length() - 1
    position = clus_position(axes)
    member = (position >> low_bit) & (members - 1)
    group = [group_ref[p] for p in range(members)]
    if top_in_ref is None:
        top = jnp.zeros(top_ref.shape[1:], jnp.float32)
    else:
        top = top_in_ref[0]
    factors = group
    for level in range(levels):
        nodes = [[factors[2 * i], factors[2 * i + 1]] for i in range(len(factors) // 2)]
        results = factor_nodes(nodes, keep_inverse=True)
        node = member >> (level + 1)
        mine_low, mine_high, mine_inverse, mine_scale = nodes[0][0], nodes[0][1], results[0][0], results[0][2]
        for i in range(1, len(nodes)):
            pick = node == i
            mine_low = jnp.where(pick, nodes[i][0], mine_low)
            mine_high = jnp.where(pick, nodes[i][1], mine_high)
            mine_inverse = jnp.where(pick, results[i][0], mine_inverse)
            mine_scale = jnp.where(pick, results[i][2], mine_scale)
        level_bit = low_bit + level
        owned = position % (2 << level_bit) == 1 << level_bit
        transfer = jnp.concatenate([mm(mine_low, mine_inverse) / mine_scale, mm(mine_high, mine_inverse) / mine_scale], axis=0)
        top = jnp.where(owned, transfer, top)
        factors = [r for _, r, _ in results]
    top_ref[0] = top
    for p in range(next_ref.shape[0]):
        next_ref[p] = factors[0]


def local_call(leaf_slot, partial_value, other_value, spread):
    leaf_count, rows, width = partial_value.shape
    vmem = pltpu.MemorySpace.VMEM
    return pl.pallas_call(
        local_kernel,
        out_shape=(
            jax.ShapeDtypeStruct((leaf_count, rows, width), jnp.float32),
            jax.ShapeDtypeStruct((leaf_count - 1, 2 * width, width), jnp.float32),
            jax.ShapeDtypeStruct((spread, width, width), jnp.float32),
        ),
        in_specs=[pl.BlockSpec(memory_space=pltpu.MemorySpace.SMEM), pl.BlockSpec(memory_space=vmem), pl.BlockSpec(memory_space=vmem)],
        out_specs=tuple(pl.BlockSpec(memory_space=vmem) for _ in range(3)),
    )(leaf_slot, partial_value, other_value)


def round_call(low_bit, axes, group, top_in, spread):
    width = group.shape[2]
    vmem = pltpu.MemorySpace.VMEM
    operands = [group] if top_in is None else [group, top_in]
    return pl.pallas_call(
        functools.partial(round_kernel, low_bit, axes),
        out_shape=(
            jax.ShapeDtypeStruct((1, 2 * width, width), jnp.float32),
            jax.ShapeDtypeStruct((spread, width, width), jnp.float32),
        ),
        in_specs=[pl.BlockSpec(memory_space=vmem) for _ in operands],
        out_specs=(pl.BlockSpec(memory_space=vmem), pl.BlockSpec(memory_space=vmem)),
    )(*operands)


def round_widths(count):
    depth = count.bit_length() - 1
    return [ROUND_BITS] * (depth // ROUND_BITS) + ([depth % ROUND_BITS] if depth % ROUND_BITS else [])


def body(axes, samples, sketch, leaf_slot):
    columns = sketch.shape[1]
    leaf_count = leaf_slot.shape[1]
    partial_value = jnp.dot(samples, sketch, precision=lax.Precision.HIGH).reshape(leaf_count, -1, columns)
    other_value = from_xor(partial_value, "samp", 1)
    order = list(reversed(axes))
    sizes = [lax.axis_size(name) for name in order] + [1]
    leaf_basis, local_transfer, factors = local_call(leaf_slot, partial_value, other_value, sizes[0])
    top_out = None
    low_bit = 0
    for index, name in enumerate(order):
        group = lax.all_to_all(factors, name, 0, 0, tiled=True)
        top_out, factors = round_call(low_bit, axes, group, top_out, sizes[index + 1])
        low_bit += sizes[index].bit_length() - 1
    return (leaf_basis.reshape(-1, columns), local_transfer, top_out, factors[0])


def solution(mesh):
    clus = mesh.shape["clus"]
    widths = round_widths(clus)
    axes = tuple(f"clus{i}" for i in range(len(widths)))
    sizes = tuple(1 << w for w in reversed(widths))
    devices = mesh.devices.reshape(sizes + (mesh.shape["samp"],))
    split = jax.sharding.Mesh(devices, axes + ("samp",))
    return jax.shard_map(
        functools.partial(body, axes),
        mesh=split,
        in_specs=(P(axes, "samp"), P("samp", None), P(axes, None)),
        out_specs=(P(axes, None), P(axes, None, None), P(axes, None, None), P()),
        check_vma=False,
    )
```

```python
import functools

import jax
import jax.numpy as jnp
from jax import lax
from jax.experimental import pallas as pl
from jax.experimental.pallas import tpu as pltpu
from jax.sharding import PartitionSpec as P

NS_STEPS = 5
ROUND_BITS = 3


highest = lax.Precision.HIGHEST


def from_xor(block, axis, mask):
    count = lax.axis_size(axis)
    route = [(low, low ^ mask) for low in range(count) if low ^ mask < count]
    return lax.ppermute(block, axis, route)


def mm(a, b):
    a_high = a.astype(jnp.bfloat16)
    a_low = (a - a_high.astype(jnp.float32)).astype(jnp.bfloat16)
    b_high = b.astype(jnp.bfloat16)
    b_low = (b - b_high.astype(jnp.float32)).astype(jnp.bfloat16)
    dot = functools.partial(jnp.dot, preferred_element_type=jnp.float32)
    return dot(a_high, b_high) + (dot(a_high, b_low) + dot(a_low, b_high))


def gram(a):
    high = a.astype(jnp.bfloat16)
    low = (a - high.astype(jnp.float32)).astype(jnp.bfloat16)
    dims = (((0,), (0,)), ((), ()))
    dot = functools.partial(lax.dot_general, dimension_numbers=dims, preferred_element_type=jnp.float32)
    return dot(high, high) + (dot(high, low) + dot(low, high))


def factor_nodes(nodes, keep_inverse=False):
    width = nodes[0][0].shape[1]
    rows = lax.broadcasted_iota(jnp.int32, (width, width), 0)
    cols = lax.broadcasted_iota(jnp.int32, (width, width), 1)
    diag = rows == cols
    identity = jnp.where(diag, 1.0, 0.0).astype(jnp.float32)
    grams = []
    for parts in nodes:
        g = gram(parts[0])
        for part in parts[1:]:
            g = g + gram(part)
        grams.append(g)
    scales = []
    for parts in nodes:
        c = jnp.sum(parts[0] * parts[0], keepdims=True)
        for part in parts[1:]:
            c = c + jnp.sum(part * part, keepdims=True)
        scales.append(c + 1e-06)
    roots = [g * (1.0 / c) for g, c in zip(grams, scales)]
    middles = [1.5 * identity - 0.5 * y for y in roots]
    roots = [mm(y, m) for y, m in zip(roots, middles)]
    inverses = middles
    finals = [None for _ in nodes]
    for step in range(NS_STEPS - 1):
        middles = [1.5 * identity - 0.5 * mm(w, y) for w, y in zip(inverses, roots)]
        roots = [mm(y, m) for y, m in zip(roots, middles)]
        if step < NS_STEPS - 2:
            inverses = [mm(m, w) for m, w in zip(middles, inverses)]
        else:
            finals = middles
    results = []
    for parts, c, y, w, last in zip(nodes, scales, roots, inverses, finals):
        s = jnp.sqrt(c)
        if keep_inverse:
            results.append((w, y * s, s, last))
        else:
            results.append(([apply_inverse(part, w, last) / s for part in parts], y * s))
    return results


def apply_inverse(part, inverse, last):
    product = mm(part, inverse)
    return product if last is None else mm(product, last)


def pair_levels(factors, levels, store):
    for level in range(levels):
        nodes = [[factors[2 * i], factors[2 * i + 1]] for i in range(len(factors) // 2)]
        results = factor_nodes(nodes)
        for i, (q_parts, _) in enumerate(results):
            store(level, i, q_parts)
        factors = [r for _, r in results]
    return factors


def local_kernel(slot_ref, z_ref, other_ref, basis_ref, transfer_ref, top_ref):
    leaf_count = z_ref.shape[0]
    width = z_ref.shape[2]
    results = factor_nodes([[z_ref[i] + other_ref[i]] for i in range(leaf_count)])
    for i, (q_parts, _) in enumerate(results):
        basis_ref[i] = q_parts[0]
    triangles = [r for _, r in results]
    factors = []
    for j in range(leaf_count):
        pick = slot_ref[0, j]
        chosen = triangles[0]
        for i in range(1, leaf_count):
            chosen = jnp.where(pick == i, triangles[i], chosen)
        factors.append(chosen)
    offsets = []
    count = leaf_count
    total = 0
    while count > 1:
        count //= 2
        offsets.append(total)
        total += count

    def store(level, i, q_parts):
        for p, part in enumerate(q_parts):
            transfer_ref[offsets[level] + i, p * width:(p + 1) * width, :] = part

    factors = pair_levels(factors, len(offsets), store)
    for p in range(top_ref.shape[0]):
        top_ref[p] = factors[0]


def clus_position(axes):
    position = 0
    for name in axes:
        position = position * lax.axis_size(name) + lax.axis_index(name)
    return position


def round_kernel(low_bit, axes, group_ref, *refs):
    top_in_ref, top_ref, next_ref = refs if len(refs) == 3 else (None,) + refs
    members = group_ref.shape[0]
    levels = members.bit_length() - 1
    position = clus_position(axes)
    member = (position >> low_bit) & (members - 1)
    group = [group_ref[p] for p in range(members)]
    if top_in_ref is None:
        top = jnp.zeros(top_ref.shape[1:], jnp.float32)
    else:
        top = top_in_ref[0]
    factors = group
    for level in range(levels):
        nodes = [[factors[2 * i], factors[2 * i + 1]] for i in range(len(factors) // 2)]
        results = factor_nodes(nodes, keep_inverse=True)
        node = member >> (level + 1)
        mine_low, mine_high, mine_inverse, mine_scale, mine_last = nodes[0][0], nodes[0][1], results[0][0], results[0][2], results[0][3]
        for i in range(1, len(nodes)):
            pick = node == i
            mine_low = jnp.where(pick, nodes[i][0], mine_low)
            mine_high = jnp.where(pick, nodes[i][1], mine_high)
            mine_inverse = jnp.where(pick, results[i][0], mine_inverse)
            mine_scale = jnp.where(pick, results[i][2], mine_scale)
            if mine_last is not None:
                mine_last = jnp.where(pick, results[i][3], mine_last)
        level_bit = low_bit + level
        owned = position % (2 << level_bit) == 1 << level_bit
        transfer = jnp.concatenate(
            [apply_inverse(mine_low, mine_inverse, mine_last) / mine_scale, apply_inverse(mine_high, mine_inverse, mine_last) / mine_scale],
            axis=0,
        )
        top = jnp.where(owned, transfer, top)
        factors = [r for _, r, _, _ in results]
    top_ref[0] = top
    for p in range(next_ref.shape[0]):
        next_ref[p] = factors[0]


def local_call(leaf_slot, partial_value, other_value, spread):
    leaf_count, rows, width = partial_value.shape
    vmem = pltpu.MemorySpace.VMEM
    return pl.pallas_call(
        local_kernel,
        out_shape=(
            jax.ShapeDtypeStruct((leaf_count, rows, width), jnp.float32),
            jax.ShapeDtypeStruct((leaf_count - 1, 2 * width, width), jnp.float32),
            jax.ShapeDtypeStruct((spread, width, width), jnp.float32),
        ),
        in_specs=[pl.BlockSpec(memory_space=pltpu.MemorySpace.SMEM), pl.BlockSpec(memory_space=vmem), pl.BlockSpec(memory_space=vmem)],
        out_specs=tuple(pl.BlockSpec(memory_space=vmem) for _ in range(3)),
    )(leaf_slot, partial_value, other_value)


def round_call(low_bit, axes, group, top_in, spread):
    width = group.shape[2]
    vmem = pltpu.MemorySpace.VMEM
    operands = [group] if top_in is None else [group, top_in]
    return pl.pallas_call(
        functools.partial(round_kernel, low_bit, axes),
        out_shape=(
            jax.ShapeDtypeStruct((1, 2 * width, width), jnp.float32),
            jax.ShapeDtypeStruct((spread, width, width), jnp.float32),
        ),
        in_specs=[pl.BlockSpec(memory_space=vmem) for _ in operands],
        out_specs=(pl.BlockSpec(memory_space=vmem), pl.BlockSpec(memory_space=vmem)),
    )(*operands)


def round_widths(count):
    depth = count.bit_length() - 1
    return [ROUND_BITS] * (depth // ROUND_BITS) + ([depth % ROUND_BITS] if depth % ROUND_BITS else [])


def body(axes, samples, sketch, leaf_slot):
    columns = sketch.shape[1]
    leaf_count = leaf_slot.shape[1]
    partial_value = jnp.dot(samples, sketch, precision=lax.Precision.HIGH).reshape(leaf_count, -1, columns)
    other_value = from_xor(partial_value, "samp", 1)
    order = list(reversed(axes))
    sizes = [lax.axis_size(name) for name in order] + [1]
    leaf_basis, local_transfer, factors = local_call(leaf_slot, partial_value, other_value, sizes[0])
    top_out = None
    low_bit = 0
    for index, name in enumerate(order):
        group = lax.all_to_all(factors, name, 0, 0, tiled=True)
        top_out, factors = round_call(low_bit, axes, group, top_out, sizes[index + 1])
        low_bit += sizes[index].bit_length() - 1
    return (leaf_basis.reshape(-1, columns), local_transfer, top_out, factors[0])


def solution(mesh):
    clus = mesh.shape["clus"]
    widths = round_widths(clus)
    axes = tuple(f"clus{i}" for i in range(len(widths)))
    sizes = tuple(1 << w for w in reversed(widths))
    devices = mesh.devices.reshape(sizes + (mesh.shape["samp"],))
    split = jax.sharding.Mesh(devices, axes + ("samp",))
    return jax.shard_map(
        functools.partial(body, axes),
        mesh=split,
        in_specs=(P(axes, "samp"), P("samp", None), P(axes, None)),
        out_specs=(P(axes, None), P(axes, None, None), P(axes, None, None), P()),
        check_vma=False,
    )
```

```python
import functools

import jax
import jax.numpy as jnp
from jax import lax
from jax.experimental import pallas as pl
from jax.experimental.pallas import tpu as pltpu
from jax.sharding import PartitionSpec as P

NS_STEPS = 5
ROUND_BITS = 3


highest = lax.Precision.HIGHEST


def from_xor(block, axis, mask):
    count = lax.axis_size(axis)
    route = [(low, low ^ mask) for low in range(count) if low ^ mask < count]
    return lax.ppermute(block, axis, route)


def mm(a, b):
    a_high = a.astype(jnp.bfloat16)
    a_low = (a - a_high.astype(jnp.float32)).astype(jnp.bfloat16)
    b_high = b.astype(jnp.bfloat16)
    b_low = (b - b_high.astype(jnp.float32)).astype(jnp.bfloat16)
    dot = functools.partial(jnp.dot, preferred_element_type=jnp.float32)
    return dot(a_high, b_high) + (dot(a_high, b_low) + dot(a_low, b_high))


def gram(a):
    high = a.astype(jnp.bfloat16)
    low = (a - high.astype(jnp.float32)).astype(jnp.bfloat16)
    dims = (((0,), (0,)), ((), ()))
    dot = functools.partial(lax.dot_general, dimension_numbers=dims, preferred_element_type=jnp.float32)
    return dot(high, high) + (dot(high, low) + dot(low, high))


def factor_nodes(nodes, keep_inverse=False):
    width = nodes[0][0].shape[1]
    rows = lax.broadcasted_iota(jnp.int32, (width, width), 0)
    cols = lax.broadcasted_iota(jnp.int32, (width, width), 1)
    diag = rows == cols
    identity = jnp.where(diag, 1.0, 0.0).astype(jnp.float32)
    grams = []
    for parts in nodes:
        g = gram(parts[0])
        for part in parts[1:]:
            g = g + gram(part)
        grams.append(g)
    scales = []
    for parts in nodes:
        c = jnp.sum(parts[0] * parts[0], keepdims=True)
        for part in parts[1:]:
            c = c + jnp.sum(part * part, keepdims=True)
        scales.append(c + 1e-06)
    roots = [g * (1.0 / c) for g, c in zip(grams, scales)]
    middles = [1.5 * identity - 0.5 * y for y in roots]
    roots = [mm(y, m) for y, m in zip(roots, middles)]
    inverses = middles
    finals = [None for _ in nodes]
    for step in range(NS_STEPS - 1):
        middles = [1.5 * identity - 0.5 * mm(w, y) for w, y in zip(inverses, roots)]
        roots = [mm(y, m) for y, m in zip(roots, middles)]
        if step < NS_STEPS - 2:
            inverses = [mm(m, w) for m, w in zip(middles, inverses)]
        else:
            finals = middles
    results = []
    for parts, c, y, w, last in zip(nodes, scales, roots, inverses, finals):
        s = jnp.sqrt(c)
        if keep_inverse:
            results.append((w, y * s, s, last))
        else:
            results.append(([apply_inverse(part, w, last) / s for part in parts], y * s))
    return results


def apply_inverse(part, inverse, last):
    product = mm(part, inverse)
    return product if last is None else mm(product, last)


def pair_levels(factors, levels, store):
    for level in range(levels):
        nodes = [[factors[2 * i], factors[2 * i + 1]] for i in range(len(factors) // 2)]
        results = factor_nodes(nodes)
        for i, (q_parts, _) in enumerate(results):
            store(level, i, q_parts)
        factors = [r for _, r in results]
    return factors


def local_kernel(slot_ref, z_ref, other_ref, basis_ref, transfer_ref, top_ref):
    leaf_count = z_ref.shape[0]
    width = z_ref.shape[2]
    results = factor_nodes([[z_ref[i] + other_ref[i]] for i in range(leaf_count)])
    for i, (q_parts, _) in enumerate(results):
        basis_ref[i] = q_parts[0]
    triangles = [r for _, r in results]
    factors = []
    for j in range(leaf_count):
        pick = slot_ref[0, j]
        chosen = triangles[0]
        for i in range(1, leaf_count):
            chosen = jnp.where(pick == i, triangles[i], chosen)
        factors.append(chosen)
    offsets = []
    count = leaf_count
    total = 0
    while count > 1:
        count //= 2
        offsets.append(total)
        total += count

    def store(level, i, q_parts):
        for p, part in enumerate(q_parts):
            transfer_ref[offsets[level] + i, p * width:(p + 1) * width, :] = part

    factors = pair_levels(factors, len(offsets), store)
    for p in range(top_ref.shape[0]):
        top_ref[p] = factors[0]


def clus_position(axes):
    position = 0
    for name in axes:
        position = position * lax.axis_size(name) + lax.axis_index(name)
    return position


def round_kernel(low_bit, axes, group_ref, *refs):
    refs, (spread_ref, sem) = refs[:-2], refs[-2:]
    top_in_ref, top_ref, next_ref = refs if len(refs) == 3 else (None,) + refs
    members = group_ref.shape[0]
    levels = members.bit_length() - 1
    position = clus_position(axes)
    member = (position >> low_bit) & (members - 1)
    group = [group_ref[p] for p in range(members)]
    if top_in_ref is None:
        top = jnp.zeros(top_ref.shape[1:], jnp.float32)
    else:
        top = top_in_ref[0]
    factors = group
    for level in range(levels):
        nodes = [[factors[2 * i], factors[2 * i + 1]] for i in range(len(factors) // 2)]
        results = factor_nodes(nodes, keep_inverse=True)
        factors = [r for _, r, _, _ in results]
        if level == levels - 1:
            for p in range(spread_ref.shape[0]):
                spread_ref[p] = factors[0]
            send = pltpu.make_async_copy(spread_ref, next_ref, sem)
            send.start()
        node = member >> (level + 1)
        mine_low, mine_high, mine_inverse, mine_scale, mine_last = nodes[0][0], nodes[0][1], results[0][0], results[0][2], results[0][3]
        for i in range(1, len(nodes)):
            pick = node == i
            mine_low = jnp.where(pick, nodes[i][0], mine_low)
            mine_high = jnp.where(pick, nodes[i][1], mine_high)
            mine_inverse = jnp.where(pick, results[i][0], mine_inverse)
            mine_scale = jnp.where(pick, results[i][2], mine_scale)
            if mine_last is not None:
                mine_last = jnp.where(pick, results[i][3], mine_last)
        level_bit = low_bit + level
        owned = position % (2 << level_bit) == 1 << level_bit
        transfer = jnp.concatenate(
            [apply_inverse(mine_low, mine_inverse, mine_last) / mine_scale, apply_inverse(mine_high, mine_inverse, mine_last) / mine_scale],
            axis=0,
        )
        top = jnp.where(owned, transfer, top)
    top_ref[0] = top
    send.wait()


def local_call(leaf_slot, partial_value, other_value, spread):
    leaf_count, rows, width = partial_value.shape
    vmem = pltpu.MemorySpace.VMEM
    return pl.pallas_call(
        local_kernel,
        out_shape=(
            jax.ShapeDtypeStruct((leaf_count, rows, width), jnp.float32),
            jax.ShapeDtypeStruct((leaf_count - 1, 2 * width, width), jnp.float32),
            jax.ShapeDtypeStruct((spread, width, width), jnp.float32),
        ),
        in_specs=[pl.BlockSpec(memory_space=pltpu.MemorySpace.SMEM), pl.BlockSpec(memory_space=vmem), pl.BlockSpec(memory_space=vmem)],
        out_specs=tuple(pl.BlockSpec(memory_space=vmem) for _ in range(3)),
    )(leaf_slot, partial_value, other_value)


def round_call(low_bit, axes, group, top_in, spread):
    width = group.shape[2]
    vmem = pltpu.MemorySpace.VMEM
    operands = [group] if top_in is None else [group, top_in]
    return pl.pallas_call(
        functools.partial(round_kernel, low_bit, axes),
        out_shape=(
            jax.ShapeDtypeStruct((1, 2 * width, width), jnp.float32),
            jax.ShapeDtypeStruct((spread, width, width), jnp.float32),
        ),
        in_specs=[pl.BlockSpec(memory_space=vmem) for _ in operands],
        out_specs=(pl.BlockSpec(memory_space=vmem), pl.BlockSpec(memory_space=pl.ANY)),
        scratch_shapes=[pltpu.VMEM((spread, width, width), jnp.float32), pltpu.SemaphoreType.DMA(())],
    )(*operands)


def round_widths(count):
    depth = count.bit_length() - 1
    return [ROUND_BITS] * (depth // ROUND_BITS) + ([depth % ROUND_BITS] if depth % ROUND_BITS else [])


def body(axes, samples, sketch, leaf_slot):
    columns = sketch.shape[1]
    leaf_count = leaf_slot.shape[1]
    partial_value = jnp.dot(samples, sketch, precision=lax.Precision.HIGH).reshape(leaf_count, -1, columns)
    other_value = from_xor(partial_value, "samp", 1)
    order = list(reversed(axes))
    sizes = [lax.axis_size(name) for name in order] + [1]
    leaf_basis, local_transfer, factors = local_call(leaf_slot, partial_value, other_value, sizes[0])
    top_out = None
    low_bit = 0
    for index, name in enumerate(order):
        group = lax.all_to_all(factors, name, 0, 0, tiled=True)
        top_out, factors = round_call(low_bit, axes, group, top_out, sizes[index + 1])
        low_bit += sizes[index].bit_length() - 1
    return (leaf_basis.reshape(-1, columns), local_transfer, top_out, factors[0])


def solution(mesh):
    clus = mesh.shape["clus"]
    widths = round_widths(clus)
    axes = tuple(f"clus{i}" for i in range(len(widths)))
    sizes = tuple(1 << w for w in reversed(widths))
    devices = mesh.devices.reshape(sizes + (mesh.shape["samp"],))
    split = jax.sharding.Mesh(devices, axes + ("samp",))
    return jax.shard_map(
        functools.partial(body, axes),
        mesh=split,
        in_specs=(P(axes, "samp"), P("samp", None), P(axes, None)),
        out_specs=(P(axes, None), P(axes, None, None), P(axes, None, None), P()),
        check_vma=False,
    )
```
